128 devices in a mesh: seq: 32 (over x, z, core), grp: 4 (over y).
Axes of the slice: x: 4, y: 4, z: 4, core: 2. Of those that a mesh axis runs over, the one named last changes fastest.
Arguments:
- queries: bfloat16 [65536, 768], P(('grp', 'seq')), parts along dimension 0, may hold values from -6 to 6
- keys: bfloat16 [65536, 768], P(('grp', 'seq')), parts along dimension 0, may hold values from -6 to 6
- values: bfloat16 [65536, 768], P(('grp', 'seq')), parts along dimension 0, may hold values from -6.5 to 6.5
- out_grad: bfloat16 [65536, 768], P(('grp', 'seq')), parts along dimension 0, may hold values from -6 to 6
- random_blocks: int32 [1024, 12, 3], P(('grp', 'seq')), parts along dimension 0, may hold values from 0 to 255, as said below
- global_blocks: int32 [8], P('grp'), parts along dimension 0, may hold values from 0 to 255, as said below
Outputs:
- attended: bfloat16 [65536, 768], P(('grp', 'seq')), parts along dimension 0
- query_grad: bfloat16 [65536, 768], P(('grp', 'seq')), parts along dimension 0
- key_grad: bfloat16 [65536, 768], P(('grp', 'seq')), parts along dimension 0
- value_grad: bfloat16 [65536, 768], P(('grp', 'seq')), parts along dimension 0
The draws below stay inside these ranges and needn't reach their ends.
There are 4 independent parts, one for each index of `grp`. The reference program is written for one: setup_inputs(seed, part) draws one part's arguments, and reference() takes and returns one part's arrays. A program takes and returns all parts, laid end to end along the dimension named above; each array names one. Nothing has to cross between parts.
Inputs may be any that keep to these rules, and one draw needn't show every extreme that they name: `random_blocks`: each entry lies on a device other than that of the query block; the 3 entries of one query block and head are distinct; of all entries of the blocks of one device, at most 14 lie on any one device, and exactly 14 on some device, for every device. `global_blocks`: two distinct block numbers, one of which is the last block 255.
All inputs are finite; a program needn't handle non-finite values.
Results may differ from the reference program's by a relative error of at most 0.03.
Values may be sent and summed in bfloat16 or wider, within the bound.
No kernel may reach another device: no remote copies, remote signals or barrier semaphores. Data moves between devices by JAX's collectives and lax.ppermute only.
A program may use at most 384 MiB of HBM per device.

```python
import math
import jax
import jax.numpy as jnp
from jax import lax

D = 768
H = 12
HD = 64
BLK = 64
R = 3
NG = 2
SLOTS = 8
SEQ_LEN = 16384
NBLK = 256
QB_DEV = 8
RAND_CAP = 14
N_SEQ = 32


def draw_queries(key, part):
    own_key = jax.random.fold_in(key, 1)
    drawn = jnp.clip(jax.random.normal(own_key, (SEQ_LEN, D), jnp.float32), -6.0, 6.0)
    return drawn.astype(jnp.bfloat16)


def draw_keys(key, part):
    own_key = jax.random.fold_in(key, 2)
    drawn = jnp.clip(jax.random.normal(own_key, (SEQ_LEN, D), jnp.float32), -6.0, 6.0)
    return drawn.astype(jnp.bfloat16)


def draw_values(key, part):
    own_key = jax.random.fold_in(key, 3)
    drawn = jnp.clip(jax.random.normal(own_key, (SEQ_LEN, D), jnp.float32), -6.0, 6.0)
    return drawn.astype(jnp.bfloat16)


def draw_random_blocks(key, part):
    owner_count = N_SEQ - 1
    entry_count = QB_DEV * H * R
    position = jnp.arange(entry_count, dtype=jnp.int32)
    slot_list = jnp.where(position < RAND_CAP, 0, 1 + (position - RAND_CAP) % (owner_count - 1))

    def for_device(dev_key, device):
        shuffle_key, owner_key, first_key = jax.random.split(dev_key, 3)
        shuffled = slot_list[jax.random.permutation(shuffle_key, entry_count)]
        offsets = 1 + jax.random.permutation(owner_key, owner_count)[shuffled]
        owner_dev = (device + offsets) % N_SEQ
        first_one = jax.random.randint(first_key, (QB_DEV, H, 1), 0, QB_DEV)
        within = (first_one + jnp.arange(R, dtype=jnp.int32)[None, None, :]) % QB_DEV
        return owner_dev.reshape(QB_DEV, H, R) * QB_DEV + within
    device_keys = jax.random.split(jax.random.fold_in(key, 11), N_SEQ)
    result = jax.vmap(for_device)(device_keys, jnp.arange(N_SEQ, dtype=jnp.int32))
    return result.reshape(NBLK, H, R).astype(jnp.int32)


def draw_global_blocks(key, part):
    first_key, order_key = jax.random.split(jax.random.fold_in(key, 13))
    other_id = jax.random.randint(first_key, (), 0, NBLK - 1)
    last_id = jnp.int32(NBLK - 1)
    flip = jax.random.randint(order_key, (), 0, 2)
    first_out = jnp.where(flip == 1, last_id, other_id)
    second_out = jnp.where(flip == 1, other_id, last_id)
    return jnp.stack([first_out, second_out]).astype(jnp.int32)


def block_scale(key, shape, pieces, least, high):
    def one(dim, parts):
        steps = jax.random.uniform(jax.random.fold_in(jax.random.fold_in(key, 6), dim), (parts,), jnp.float32, least / len(pieces), high / len(pieces))
        return jnp.repeat(jnp.exp(steps), shape[dim] // parts).reshape((-1,) + (1,) * (len(shape) - dim - 1))

    factor_of = one(*pieces[0])
    for cut in pieces[1:]:
        factor_of = factor_of * one(*cut)
    return factor_of


def centred(rng, extent, deviation, reach, shards=(), kind=jnp.bfloat16):
    drawn = deviation * jax.random.normal(rng, extent, jnp.float32)
    if shards:
        drawn = drawn * block_scale(rng, extent, shards, -0.22, 0.18)
    return jnp.clip(drawn, -reach, reach).astype(kind)


def setup_inputs(seed: int = 0, part: int = 0) -> dict:
    streams_of = jax.random.split(jax.random.key(seed), 7)
    own_keys = jax.random.split(jax.random.fold_in(streams_of[6], part), 7)
    return {
        "queries": draw_queries(jax.random.fold_in(jax.random.fold_in(streams_of[6], part), 71), part),
        "keys": draw_keys(jax.random.fold_in(jax.random.fold_in(streams_of[6], part), 71), part),
        "values": draw_values(jax.random.fold_in(jax.random.fold_in(streams_of[6], part), 71), part),
        "out_grad": centred(own_keys[3], (SEQ_LEN, D), 1.0, 6.0, ((0, 32),)),
        "random_blocks": draw_random_blocks(jax.random.fold_in(jax.random.fold_in(streams_of[6], part), 71), part),
        "global_blocks": draw_global_blocks(jax.random.fold_in(jax.random.fold_in(streams_of[6], part), 71), part),
    }


def rounded(values_f):
    return lax.optimization_barrier(values_f.astype(jnp.bfloat16)).astype(jnp.float32)

def to_blocks(matrix):
    return matrix.reshape(NBLK, BLK, H, HD).transpose(0, 2, 1, 3)

def from_blocks(blocked):
    return blocked.transpose(0, 2, 1, 3).reshape(NBLK * BLK, H * HD)

def sparse_block(query_b, grad_b, keyval_b, allowed, factor):
    query_f = query_b.astype(jnp.float32)
    grad_f = grad_b.astype(jnp.float32)
    key_f = keyval_b[..., :HD].astype(jnp.float32)
    value_f = keyval_b[..., HD:].astype(jnp.float32)
    scores = jnp.einsum('hqd,hkd->hqk', query_f, key_f) * factor
    mask = allowed[:, None, :]
    row_max = lax.optimization_barrier(jnp.max(jnp.where(mask, scores, -1e+30), axis=-1, keepdims=True))
    expo = jnp.where(mask, jnp.exp(scores - row_max), 0.0)
    totals = lax.optimization_barrier(jnp.sum(expo, axis=-1, keepdims=True))
    result = jnp.einsum('hqk,hkd->hqd', rounded(expo), value_f) / totals
    probs = expo / totals
    dprobs = jnp.einsum('hqd,hkd->hqk', grad_f, value_f)
    dotted = lax.optimization_barrier(jnp.sum(grad_f * result, axis=-1, keepdims=True))
    dscore = rounded(probs * (dprobs - dotted))
    dquery = factor * jnp.einsum('hqk,hkd->hqd', dscore, key_f)
    dkey = factor * jnp.einsum('hqk,hqd->hkd', dscore, query_f)
    dvalue = jnp.einsum('hqk,hqd->hkd', rounded(probs), grad_f)
    return (result, dquery, jnp.concatenate([dkey, dvalue], axis=-1))

def reference(queries, keys, values, out_grad, random_blocks, global_blocks):
    factor = 1.0 / math.sqrt(HD)
    block_ids = jnp.arange(NBLK, dtype=jnp.int32)
    is_global = jnp.any(block_ids[:, None] == global_blocks[None, :], axis=1)
    row_global = jnp.repeat(is_global, BLK)
    masked = jnp.where(row_global[:, None], jnp.zeros_like(out_grad), out_grad)
    query_h = to_blocks(queries)
    grad_h = to_blocks(masked)
    keyval_h = jnp.concatenate([to_blocks(keys), to_blocks(values)], axis=-1)
    head_ids = jnp.arange(H, dtype=jnp.int32)
    shifts = jnp.arange(-1, 2, dtype=jnp.int32)

    def step(accum, block):
        window = (block + shifts) % NBLK
        window_h = jnp.broadcast_to(window[None, :], (H, 3))
        chosen = random_blocks[block]
        key_ids = jnp.concatenate([window_h, jnp.broadcast_to(global_blocks[None, :], (H, NG)), chosen], axis=1)
        others = jnp.concatenate([window_h, chosen], axis=1)
        global_kept = jnp.all(global_blocks[None, :, None] != others[:, None, :], axis=2)
        allowed = jnp.concatenate([jnp.ones((H, 3), jnp.bool_), global_kept, jnp.ones((H, R), jnp.bool_)], axis=1)
        picked = keyval_h[key_ids, head_ids[:, None]]
        result, dquery, terms = sparse_block(query_h[block], grad_h[block], picked.reshape(H, SLOTS * BLK, 2 * HD), jnp.repeat(allowed, BLK, axis=1), factor)
        terms = terms.reshape(H, SLOTS, BLK, 2 * HD)
        accum = accum.at[key_ids[:, :3 + NG], head_ids[:, None]].add(terms[:, :3 + NG])
        accum = accum.at[key_ids[:, 3 + NG:], head_ids[:, None]].add(rounded(terms[:, 3 + NG:]))
        return (accum, (result, dquery))
    accum0 = jnp.zeros((NBLK, H, BLK, 2 * HD), jnp.float32)
    accum, (results, dqueries) = lax.scan(step, accum0, block_ids)
    attended = from_blocks(results)
    query_sum = from_blocks(dqueries)
    key_all = keys.astype(jnp.float32).reshape(SEQ_LEN, H, HD)
    value_all = values.astype(jnp.float32).reshape(SEQ_LEN, H, HD)
    dkey_all = jnp.zeros((SEQ_LEN, H, HD), jnp.float32)
    dvalue_all = jnp.zeros((SEQ_LEN, H, HD), jnp.float32)
    for number in range(NG):
        row_start = global_blocks[number] * BLK
        query_g = lax.dynamic_slice_in_dim(queries, row_start, BLK, 0).astype(jnp.float32).reshape(BLK, H, HD)
        grad_g = lax.dynamic_slice_in_dim(out_grad, row_start, BLK, 0).astype(jnp.float32).reshape(BLK, H, HD)
        scores = jnp.einsum('qhd,khd->hqk', query_g, key_all) * factor
        row_max = lax.optimization_barrier(jnp.max(scores, axis=-1, keepdims=True))
        expo = jnp.exp(scores - row_max)
        totals = lax.optimization_barrier(jnp.sum(expo, axis=-1, keepdims=True))
        result = jnp.einsum('hqk,khd->hqd', rounded(expo), value_all) / totals
        probs = expo / totals
        dprobs = jnp.einsum('qhd,khd->hqk', grad_g, value_all)
        dotted = lax.optimization_barrier(jnp.sum(grad_g.transpose(1, 0, 2) * result, axis=-1, keepdims=True))
        dscore = rounded(probs * (dprobs - dotted))
        dquery = factor * jnp.einsum('hqk,khd->qhd', dscore, key_all)
        dkey_all = dkey_all + factor * jnp.einsum('hqk,qhd->khd', dscore, query_g)
        dvalue_all = dvalue_all + jnp.einsum('hqk,qhd->khd', rounded(probs), grad_g)
        attended = lax.dynamic_update_slice_in_dim(attended, result.transpose(1, 0, 2).reshape(BLK, D), row_start, 0)
        current = lax.dynamic_slice_in_dim(query_sum, row_start, BLK, 0)
        query_sum = lax.dynamic_update_slice_in_dim(query_sum, current + dquery.reshape(BLK, D), row_start, 0)
    key_grad = from_blocks(accum[..., :HD]) + dkey_all.reshape(SEQ_LEN, D)
    value_grad = from_blocks(accum[..., HD:]) + dvalue_all.reshape(SEQ_LEN, D)
    return (attended.astype(jnp.bfloat16), query_sum.astype(jnp.bfloat16), key_grad.astype(jnp.bfloat16), value_grad.astype(jnp.bfloat16))
```

```python
import math

import jax
import jax.numpy as jnp
from jax import lax
from jax.sharding import PartitionSpec as P

H = 12
HD = 64
BLK = 64
R = 3
NG = 2
QGROUP = 8
SLOTS = 8


def padded_2(block, sides, width):
    for axis, dim in sides:
        count = lax.axis_size(axis)
        forward = [(i, i + 1) for i in range(count - 1)]
        forward.append((count - 1, 0))
        backward = [(target, source) for source, target in forward]
        low = lax.ppermute(
            lax.slice_in_dim(block, block.shape[dim] - width, None, axis=dim), axis, forward
        )
        high = lax.ppermute(lax.slice_in_dim(block, 0, width, axis=dim), axis, backward)
        block = jnp.concatenate([low, block, high], axis=dim)
    return block


def from_owners(value, owners):
    devices = lax.axis_size("seq")
    count = value.shape[0]
    chunks = value.reshape(count, devices, -1).transpose(1, 0, 2)
    got = lax.all_to_all(chunks, "seq", 0, 0, tiled=True)
    mine = jnp.stack([got[owners[i], i] for i in range(count)])
    full = lax.all_gather(mine, "seq", axis=0, tiled=False)
    return full.transpose(1, 0, 2).reshape(value.shape)


def summed_to_all(value):
    devices = lax.axis_size("seq")
    chunks = value.astype(jnp.bfloat16).reshape(devices, -1)
    got = lax.all_to_all(chunks, "seq", 0, 0, tiled=True)
    total = jnp.sum(got.astype(jnp.float32), axis=0).astype(jnp.bfloat16)
    full = lax.all_gather(total, "seq", axis=0, tiled=True)
    return full.reshape(value.shape).astype(jnp.float32)


def head_blocks(matrix, blocks):
    return matrix.reshape(blocks, BLK, H, HD).transpose(0, 2, 1, 3)


def token_rows(blocked):
    blocks = blocked.shape[0]
    return blocked.transpose(0, 2, 1, 3).reshape(blocks * BLK, H * HD)


def pair_heads(rows, blocks):
    return (
        rows.reshape(blocks, BLK, 2, H, HD).transpose(0, 3, 1, 2, 4).reshape(blocks, H, BLK, 2 * HD)
    )


def slot_plan(block_lists, per_dev, devices, head_ids):
    owners = (block_lists // per_dev).reshape(-1)
    req_codes = (block_lists % per_dev * H + head_ids[None, :, None]).reshape(-1)
    onehot = (owners[:, None] == jnp.arange(devices, dtype=jnp.int32)[None, :]).astype(jnp.int32)
    before = jnp.cumsum(onehot, axis=0) - onehot
    return (owners, jnp.sum(before * onehot, axis=1), req_codes)


def sparse_group(query_g, grad_g, keyvals, allowed, factor):
    key_part = keyvals[..., :HD]
    value_part = keyvals[..., HD:]
    scores = (
        jnp.einsum("ghqd,ghkd->ghqk", query_g, key_part, preferred_element_type=jnp.float32)
        * factor
    )
    mask = allowed[:, :, None, :]
    row_max = jnp.max(jnp.where(mask, scores, -1e30), axis=-1, keepdims=True)
    expo = jnp.where(mask, jnp.exp(scores - row_max), 0.0)
    totals = jnp.sum(expo, axis=-1, keepdims=True)
    result = (
        jnp.einsum(
            "ghqk,ghkd->ghqd",
            expo.astype(jnp.bfloat16),
            value_part,
            preferred_element_type=jnp.float32,
        )
        / totals
    )
    probs = expo / totals
    dprobs = jnp.einsum("ghqd,ghkd->ghqk", grad_g, value_part, preferred_element_type=jnp.float32)
    dotted = jnp.sum(grad_g.astype(jnp.float32) * result, axis=-1, keepdims=True)
    dscore = (probs * (dprobs - dotted)).astype(jnp.bfloat16)
    dquery = factor * jnp.einsum(
        "ghqk,ghkd->ghqd", dscore, key_part, preferred_element_type=jnp.float32
    )
    dkey = factor * jnp.einsum(
        "ghqk,ghqd->ghkd", dscore, query_g, preferred_element_type=jnp.float32
    )
    dvalue = jnp.einsum(
        "ghqk,ghqd->ghkd", probs.astype(jnp.bfloat16), grad_g, preferred_element_type=jnp.float32
    )
    stats = jnp.stack([row_max[..., 0], totals[..., 0], dotted[..., 0]], axis=1)
    return (result, dquery, jnp.concatenate([dkey, dvalue], axis=-1), stats)


def per_device(queries, keys, values, out_grad, random_blocks, global_blocks):
    tokens = queries.shape[0]
    width = queries.shape[1]
    per_dev = tokens // BLK
    devices = lax.axis_size("seq")
    me_index = lax.axis_index("seq")
    blocks_all = per_dev * devices
    factor = 1.0 / math.sqrt(HD)
    entry_count = per_dev * H * R
    capacity = (entry_count + devices - 2) // (devices - 1) + 4
    head_ids = jnp.arange(H, dtype=jnp.int32)
    block_ids = me_index * per_dev + jnp.arange(per_dev, dtype=jnp.int32)
    is_global = jnp.any(block_ids[:, None] == global_blocks[None, :], axis=1)
    row_global = jnp.repeat(is_global, BLK)
    masked = jnp.where(row_global[:, None], jnp.zeros_like(out_grad), out_grad)
    kv_rows = jnp.concatenate([keys, values], axis=1)
    edge_rows = jnp.concatenate([kv_rows[:BLK], kv_rows[-BLK:]], axis=0)
    padded = padded_2(edge_rows, (("seq", 0),), BLK)
    left_rows = padded[:BLK]
    right_rows = padded[3 * BLK :]
    extended = jnp.concatenate(
        [
            left_rows[None, :, : 2 * width],
            kv_rows.reshape(per_dev, BLK, 2 * width),
            right_rows[None, :, : 2 * width],
        ],
        axis=0,
    )
    kv_heads = pair_heads(extended, per_dev + 2)
    kv_local = kv_heads[1 : per_dev + 1]
    global_rows = []
    for number in range(NG):
        row_start = global_blocks[number] % per_dev * BLK
        global_rows.append(
            jnp.concatenate(
                [
                    lax.dynamic_slice_in_dim(source, row_start, BLK, 0)
                    for source in (queries, keys, values, out_grad)
                ],
                axis=1,
            )
        )
    grows = from_owners(jnp.stack(global_rows), global_blocks // per_dev)
    g_query = grows[:, :, :width].reshape(NG, BLK, H, HD)
    g_grad = grows[:, :, 3 * width :].reshape(NG, BLK, H, HD)
    g_kv = pair_heads(grows[:, :, width : 3 * width], NG)
    owners, slot_ids, req_codes = slot_plan(random_blocks, per_dev, devices, head_ids)
    slot_key = owners * capacity + slot_ids
    slot_hit = jnp.arange(devices * capacity, dtype=jnp.int32)[:, None] == slot_key[None, :]
    outgoing = jnp.where(
        jnp.any(slot_hit, axis=1), jnp.sum(jnp.where(slot_hit, req_codes[None, :], 0), axis=1), -1
    ).reshape(devices, capacity)
    wanted = lax.all_to_all(outgoing, "seq", split_axis=0, concat_axis=0, tiled=True)
    sending = kv_local.reshape(per_dev * H, BLK, 2 * HD)[jnp.maximum(wanted, 0)]
    fetched = lax.all_to_all(sending, "seq", split_axis=0, concat_axis=0, tiled=True)
    rand_kv = fetched[owners, slot_ids].reshape(per_dev, H, R, BLK, 2 * HD)
    shifts = jnp.arange(-1, 2, dtype=jnp.int32)
    window_ids = (block_ids[:, None] + shifts[None, :]) % blocks_all
    other_ids = jnp.concatenate(
        [jnp.broadcast_to(window_ids[:, None, :], (per_dev, H, 3)), random_blocks], axis=2
    )
    global_kept = jnp.all(global_blocks[None, None, :, None] != other_ids[:, :, None, :], axis=3)
    allowed = jnp.concatenate(
        [jnp.ones((per_dev, H, 3), jnp.bool_), global_kept, jnp.ones((per_dev, H, R), jnp.bool_)],
        axis=2,
    )
    allowed = jnp.repeat(allowed, BLK, axis=2)
    query_heads = head_blocks(queries, per_dev)
    grad_heads = head_blocks(masked, per_dev)
    group = QGROUP
    groups = per_dev // group
    glob_slots = jnp.broadcast_to(g_kv.transpose(1, 0, 2, 3)[None], (group, H, NG, BLK, 2 * HD))

    def run_group(number):
        win_slots = jnp.stack(
            [kv_heads[0:group], kv_heads[1 : group + 1], kv_heads[2 : group + 2]], axis=2
        )
        keyvals = jnp.concatenate([win_slots, glob_slots, rand_kv], axis=2).reshape(
            group, H, SLOTS * BLK, 2 * HD
        )
        result, dquery, terms, stats = sparse_group(
            query_heads, grad_heads, keyvals, allowed, factor
        )
        terms = terms.reshape(group, H, SLOTS, BLK, 2 * HD)
        spacing = ((0, 0), (0, 0), (0, 0), (0, 0))
        window_sum = (
            jnp.pad(terms[:, :, 0], ((0, 2),) + spacing[1:])
            + jnp.pad(terms[:, :, 1], ((1, 1),) + spacing[1:])
            + jnp.pad(terms[:, :, 2], ((2, 0),) + spacing[1:])
        )
        global_sum = jnp.sum(terms[:, :, 3 : 3 + NG], axis=0)
        random_out = terms[:, :, 3 + NG :].astype(jnp.bfloat16)
        return (result, dquery, window_sum, global_sum, random_out, stats)

    mapped = lax.map(run_group, jnp.arange(groups, dtype=jnp.int32))
    result = mapped[0].reshape(per_dev, H, BLK, HD)
    dquery = mapped[1].reshape(per_dev, H, BLK, HD)
    place = (
        jnp.arange(groups, dtype=jnp.int32)[:, None] * group
        + jnp.arange(group + 2, dtype=jnp.int32)[None, :]
    ).reshape(-1)
    if groups == 1:
        padded_grads = mapped[2].reshape(per_dev + 2, H, BLK, 2 * HD)
    else:
        padded_grads = (
            jnp.zeros((per_dev + 2, H, BLK, 2 * HD), jnp.float32)
            .at[place]
            .add(mapped[2].reshape(-1, H, BLK, 2 * HD))
        )
    global_part = jnp.sum(mapped[3], axis=0).transpose(1, 0, 2, 3)
    random_out = mapped[4].reshape(-1, BLK, 2 * HD)
    stats = mapped[5].reshape(per_dev, 3, H, BLK)
    own_grads = padded_grads[1 : per_dev + 1]
    edge_pair = jnp.stack([padded_grads[0], padded_grads[per_dev + 1]])
    near_grads = padded_2(edge_pair.astype(jnp.bfloat16), (("seq", 0),), 1).astype(edge_pair.dtype)
    own_grads = own_grads.at[0].add(near_grads[0]).at[per_dev - 1].add(near_grads[3])
    back_buffer = jnp.einsum(
        "se,ef->sf",
        slot_hit.astype(jnp.bfloat16),
        random_out.reshape(-1, BLK * 2 * HD),
        preferred_element_type=jnp.bfloat16,
    ).reshape(devices, capacity, BLK, 2 * HD)
    returned = lax.all_to_all(back_buffer, "seq", split_axis=0, concat_axis=0, tiled=True)
    code_hit = (
        wanted.reshape(-1)[:, None] == jnp.arange(per_dev * H, dtype=jnp.int32)[None, :]
    ).astype(jnp.bfloat16)
    table_grads = jnp.einsum(
        "sc,sf->cf",
        code_hit,
        returned.reshape(-1, BLK * 2 * HD),
        preferred_element_type=jnp.float32,
    ).reshape(per_dev * H, BLK, 2 * HD)
    own_grads = own_grads + table_grads.reshape(per_dev, H, BLK, 2 * HD)
    key_tok = keys.reshape(tokens, H, HD)
    value_tok = values.reshape(tokens, H, HD)
    scores = (
        jnp.einsum("gqhd,khd->ghqk", g_query, key_tok, preferred_element_type=jnp.float32) * factor
    )
    local_max = jnp.max(scores, axis=-1)
    local_expo = jnp.exp(scores - local_max[..., None])
    part_acc = jnp.einsum(
        "ghqk,khd->ghqd",
        local_expo.astype(jnp.bfloat16),
        value_tok,
        preferred_element_type=jnp.float32,
    )
    row_shape = local_max.shape
    packed = jnp.concatenate(
        [local_max[..., None], jnp.sum(local_expo, axis=-1)[..., None], part_acc], axis=-1
    ).reshape(devices, -1, HD + 2)
    got = lax.all_to_all(packed, "seq", 0, 0, tiled=True)
    top = jnp.max(got[..., 0], axis=0)
    scale = jnp.exp(got[..., 0] - top[None])
    tot = jnp.sum(scale * got[..., 1], axis=0)
    acc = jnp.sum(scale[..., None] * got[..., 2:], axis=0) / tot[:, None]
    merged = lax.all_gather(
        jnp.concatenate([top[:, None], tot[:, None], acc], axis=-1), "seq", axis=0, tiled=True
    )
    row_top = merged[:, 0].reshape(row_shape)
    row_tot = merged[:, 1].reshape(row_shape)
    global_out = merged[:, 2:].reshape(row_shape + (HD,))
    probs = jnp.exp(scores - row_top[..., None]) / row_tot[..., None]
    dprobs = jnp.einsum("gqhd,khd->ghqk", g_grad, value_tok, preferred_element_type=jnp.float32)
    dotted = jnp.sum(g_grad.transpose(0, 2, 1, 3).astype(jnp.float32) * global_out, axis=-1)
    dscore = (probs * (dprobs - dotted[..., None])).astype(jnp.bfloat16)
    g_dquery = factor * jnp.einsum(
        "ghqk,khd->ghqd", dscore, key_tok, preferred_element_type=jnp.float32
    )
    tok_dkey = factor * jnp.einsum(
        "ghqk,gqhd->khd", dscore, g_query, preferred_element_type=jnp.float32
    )
    tok_dvalue = jnp.einsum(
        "ghqk,gqhd->khd", probs.astype(jnp.bfloat16), g_grad, preferred_element_type=jnp.float32
    )
    both_sum = summed_to_all(jnp.concatenate([g_dquery, global_part], axis=-1))
    dquery_sum = both_sum[..., :HD]
    global_sum = both_sum[..., HD:]
    for number in range(NG):
        owned = global_blocks[number] // per_dev == me_index
        local_block = global_blocks[number] % per_dev
        result = result.at[local_block].set(
            jnp.where(owned, global_out[number], result[local_block])
        )
        dquery = dquery.at[local_block].add(jnp.where(owned, dquery_sum[number], 0.0))
        own_grads = own_grads.at[local_block].add(jnp.where(owned, global_sum[number], 0.0))
    attended = token_rows(result).astype(jnp.bfloat16)
    query_grad = token_rows(dquery).astype(jnp.bfloat16)
    key_grad = (token_rows(own_grads[..., :HD]) + tok_dkey.reshape(tokens, width)).astype(
        jnp.bfloat16
    )
    value_grad = (token_rows(own_grads[..., HD:]) + tok_dvalue.reshape(tokens, width)).astype(
        jnp.bfloat16
    )
    return (attended, query_grad, key_grad, value_grad)


def solution(mesh):
    return jax.shard_map(
        per_device,
        mesh=mesh,
        in_specs=(
            P(("grp", "seq"), None),
            P(("grp", "seq"), None),
            P(("grp", "seq"), None),
            P(("grp", "seq"), None),
            P(("grp", "seq"), None, None),
            P("grp"),
        ),
        out_specs=(
            P(("grp", "seq"), None),
            P(("grp", "seq"), None),
            P(("grp", "seq"), None),
            P(("grp", "seq"), None),
        ),
        check_vma=False,
    )
```

```python
import math

import jax
import jax.numpy as jnp
from jax import lax
from jax.experimental import pallas as pl
from jax.sharding import PartitionSpec as P

H = 12
HD = 64
BLK = 64
R = 3
NG = 2
QGROUP = 8
SLOTS = 8


def padded_2(block, sides, width):
    for axis, dim in sides:
        count = lax.axis_size(axis)
        forward = [(i, i + 1) for i in range(count - 1)]
        forward.append((count - 1, 0))
        backward = [(target, source) for source, target in forward]
        low = lax.ppermute(
            lax.slice_in_dim(block, block.shape[dim] - width, None, axis=dim), axis, forward
        )
        high = lax.ppermute(lax.slice_in_dim(block, 0, width, axis=dim), axis, backward)
        block = jnp.concatenate([low, block, high], axis=dim)
    return block


def from_owners(value, owners):
    devices = lax.axis_size("seq")
    count = value.shape[0]
    chunks = value.reshape(count, devices, -1).transpose(1, 0, 2)
    got = lax.all_to_all(chunks, "seq", 0, 0, tiled=True)
    mine = jnp.stack([got[owners[i], i] for i in range(count)])
    full = lax.all_gather(mine, "seq", axis=0, tiled=False)
    return full.transpose(1, 0, 2).reshape(value.shape)


def summed_to_all(value):
    devices = lax.axis_size("seq")
    chunks = value.astype(jnp.bfloat16).reshape(devices, -1)
    got = lax.all_to_all(chunks, "seq", 0, 0, tiled=True)
    total = jnp.sum(got.astype(jnp.float32), axis=0).astype(jnp.bfloat16)
    full = lax.all_gather(total, "seq", axis=0, tiled=True)
    return full.reshape(value.shape).astype(jnp.float32)


def head_blocks(matrix, blocks):
    return matrix.reshape(blocks, BLK, H, HD).transpose(0, 2, 1, 3)


def token_rows(blocked):
    blocks = blocked.shape[0]
    return blocked.transpose(0, 2, 1, 3).reshape(blocks * BLK, H * HD)


def pair_heads(rows, blocks):
    return (
        rows.reshape(blocks, BLK, 2, H, HD).transpose(0, 3, 1, 2, 4).reshape(blocks, H, BLK, 2 * HD)
    )


def slot_plan(block_lists, per_dev, devices, head_ids):
    owners = (block_lists // per_dev).reshape(-1)
    req_codes = (block_lists % per_dev * H + head_ids[None, :, None]).reshape(-1)
    onehot = (owners[:, None] == jnp.arange(devices, dtype=jnp.int32)[None, :]).astype(jnp.int32)
    before = jnp.cumsum(onehot, axis=0) - onehot
    return (owners, jnp.sum(before * onehot, axis=1), req_codes)


def sparse_group(query_g, grad_g, keyvals, allowed, factor):
    key_part = keyvals[..., :HD]
    value_part = keyvals[..., HD:]
    scores = (
        jnp.einsum("ghqd,ghkd->ghqk", query_g, key_part, preferred_element_type=jnp.float32)
        * factor
    )
    mask = allowed[:, :, None, :]
    row_max = jnp.max(jnp.where(mask, scores, -1e30), axis=-1, keepdims=True)
    expo = jnp.where(mask, jnp.exp(scores - row_max), 0.0)
    totals = jnp.sum(expo, axis=-1, keepdims=True)
    result = (
        jnp.einsum(
            "ghqk,ghkd->ghqd",
            expo.astype(jnp.bfloat16),
            value_part,
            preferred_element_type=jnp.float32,
        )
        / totals
    )
    probs = expo / totals
    dprobs = jnp.einsum("ghqd,ghkd->ghqk", grad_g, value_part, preferred_element_type=jnp.float32)
    dotted = jnp.sum(grad_g.astype(jnp.float32) * result, axis=-1, keepdims=True)
    dscore = (probs * (dprobs - dotted)).astype(jnp.bfloat16)
    dquery = factor * jnp.einsum(
        "ghqk,ghkd->ghqd", dscore, key_part, preferred_element_type=jnp.float32
    )
    dkey = factor * jnp.einsum(
        "ghqk,ghqd->ghkd", dscore, query_g, preferred_element_type=jnp.float32
    )
    dvalue = jnp.einsum(
        "ghqk,ghqd->ghkd", probs.astype(jnp.bfloat16), grad_g, preferred_element_type=jnp.float32
    )
    stats = jnp.stack([row_max[..., 0], totals[..., 0], dotted[..., 0]], axis=1)
    return (result, dquery, jnp.concatenate([dkey, dvalue], axis=-1), stats)


def sparse_kernel(q_ref, g_ref, kv_ref, allow_ref, out_ref, dq_ref, terms_ref, *, factor):
    query = q_ref[0, 0]
    grad = g_ref[0, 0]
    keyval = kv_ref[0, 0]
    key = keyval[:, :HD]
    value = keyval[:, HD:]
    nt = (((1,), (1,)), ((), ()))
    scores = lax.dot_general(query, key, nt, preferred_element_type=jnp.float32) * factor
    mask = allow_ref[0, 0] > 0.5
    row_max = jnp.max(jnp.where(mask, scores, -1e30), axis=-1, keepdims=True)
    expo = jnp.where(mask, jnp.exp(scores - row_max), 0.0)
    totals = jnp.sum(expo, axis=-1, keepdims=True)
    result = jnp.dot(expo.astype(jnp.bfloat16), value, preferred_element_type=jnp.float32) / totals
    probs = expo / totals
    dprobs = lax.dot_general(grad, value, nt, preferred_element_type=jnp.float32)
    dotted = jnp.sum(grad.astype(jnp.float32) * result, axis=-1, keepdims=True)
    dscore = probs * (dprobs - dotted)
    dq = factor * jnp.dot(dscore.astype(jnp.bfloat16), key, preferred_element_type=jnp.float32)
    dkey = factor * jnp.dot(dscore.T.astype(jnp.bfloat16), query, preferred_element_type=jnp.float32)
    dvalue = jnp.dot(probs.T.astype(jnp.bfloat16), grad, preferred_element_type=jnp.float32)
    out_ref[0, 0] = result
    dq_ref[0, 0] = dq
    terms_ref[0, 0, :, :HD] = dkey
    terms_ref[0, 0, :, HD:] = dvalue


def sparse_call(query_h, grad_h, keyvals, allowed_f, factor, interpret=False):
    blocks, heads, rows, _ = query_h.shape
    keys_n = keyvals.shape[2]
    small = pl.BlockSpec((1, 1, rows, HD), lambda i, h: (i, h, 0, 0))
    return pl.pallas_call(
        lambda *refs: sparse_kernel(*refs, factor=factor),
        grid=(blocks, heads),
        in_specs=[
            small,
            small,
            pl.BlockSpec((1, 1, keys_n, 2 * HD), lambda i, h: (i, h, 0, 0)),
            pl.BlockSpec((1, 1, 1, keys_n), lambda i, h: (i, h, 0, 0)),
        ],
        out_specs=[
            small,
            small,
            pl.BlockSpec((1, 1, keys_n, 2 * HD), lambda i, h: (i, h, 0, 0)),
        ],
        out_shape=[
            jax.ShapeDtypeStruct((blocks, heads, rows, HD), jnp.float32),
            jax.ShapeDtypeStruct((blocks, heads, rows, HD), jnp.float32),
            jax.ShapeDtypeStruct((blocks, heads, keys_n, 2 * HD), jnp.float32),
        ],
        interpret=interpret,
    )(query_h, grad_h, keyvals, allowed_f)


def per_device(queries, keys, values, out_grad, random_blocks, global_blocks):
    tokens = queries.shape[0]
    width = queries.shape[1]
    per_dev = tokens // BLK
    devices = lax.axis_size("seq")
    me_index = lax.axis_index("seq")
    blocks_all = per_dev * devices
    factor = 1.0 / math.sqrt(HD)
    entry_count = per_dev * H * R
    capacity = (entry_count + devices - 2) // (devices - 1) + 4
    head_ids = jnp.arange(H, dtype=jnp.int32)
    block_ids = me_index * per_dev + jnp.arange(per_dev, dtype=jnp.int32)
    is_global = jnp.any(block_ids[:, None] == global_blocks[None, :], axis=1)
    row_global = jnp.repeat(is_global, BLK)
    masked = jnp.where(row_global[:, None], jnp.zeros_like(out_grad), out_grad)
    kv_rows = jnp.concatenate([keys, values], axis=1)
    edge_rows = jnp.concatenate([kv_rows[:BLK], kv_rows[-BLK:]], axis=0)
    padded = padded_2(edge_rows, (("seq", 0),), BLK)
    left_rows = padded[:BLK]
    right_rows = padded[3 * BLK :]
    extended = jnp.concatenate(
        [
            left_rows[None, :, : 2 * width],
            kv_rows.reshape(per_dev, BLK, 2 * width),
            right_rows[None, :, : 2 * width],
        ],
        axis=0,
    )
    kv_heads = pair_heads(extended, per_dev + 2)
    kv_local = kv_heads[1 : per_dev + 1]
    global_rows = []
    for number in range(NG):
        row_start = global_blocks[number] % per_dev * BLK
        global_rows.append(
            jnp.concatenate(
                [
                    lax.dynamic_slice_in_dim(source, row_start, BLK, 0)
                    for source in (queries, keys, values, out_grad)
                ],
                axis=1,
            )
        )
    stacked_rows = jnp.stack(global_rows)
    owners, slot_ids, req_codes = slot_plan(random_blocks, per_dev, devices, head_ids)
    slot_key = owners * capacity + slot_ids
    slot_hit = jnp.arange(devices * capacity, dtype=jnp.int32)[:, None] == slot_key[None, :]
    outgoing = jnp.where(
        jnp.any(slot_hit, axis=1), jnp.sum(jnp.where(slot_hit, req_codes[None, :], 0), axis=1), -1
    ).reshape(devices, capacity)
    wanted = lax.all_to_all(outgoing, "seq", split_axis=0, concat_axis=0, tiled=True)
    sending = kv_local.reshape(per_dev * H, BLK, 2 * HD)[jnp.maximum(wanted, 0)]
    sending, stacked_rows = lax.optimization_barrier((sending, stacked_rows))
    grows = from_owners(stacked_rows, global_blocks // per_dev)
    g_query = grows[:, :, :width].reshape(NG, BLK, H, HD)
    g_grad = grows[:, :, 3 * width :].reshape(NG, BLK, H, HD)
    g_kv = pair_heads(grows[:, :, width : 3 * width], NG)
    fetched = lax.all_to_all(sending, "seq", split_axis=0, concat_axis=0, tiled=True)
    rand_kv = fetched[owners, slot_ids].reshape(per_dev, H, R, BLK, 2 * HD)
    shifts = jnp.arange(-1, 2, dtype=jnp.int32)
    window_ids = (block_ids[:, None] + shifts[None, :]) % blocks_all
    other_ids = jnp.concatenate(
        [jnp.broadcast_to(window_ids[:, None, :], (per_dev, H, 3)), random_blocks], axis=2
    )
    global_kept = jnp.all(global_blocks[None, None, :, None] != other_ids[:, :, None, :], axis=3)
    allowed = jnp.concatenate(
        [jnp.ones((per_dev, H, 3), jnp.bool_), global_kept, jnp.ones((per_dev, H, R), jnp.bool_)],
        axis=2,
    )
    allowed = jnp.repeat(allowed, BLK, axis=2)
    query_heads = head_blocks(queries, per_dev)
    grad_heads = head_blocks(masked, per_dev)
    group = QGROUP
    groups = per_dev // group
    glob_slots = jnp.broadcast_to(g_kv.transpose(1, 0, 2, 3)[None], (group, H, NG, BLK, 2 * HD))

    def run_group(number):
        win_slots = jnp.stack(
            [kv_heads[0:group], kv_heads[1 : group + 1], kv_heads[2 : group + 2]], axis=2
        )
        keyvals = jnp.concatenate([win_slots, glob_slots, rand_kv], axis=2).reshape(
            group, H, SLOTS * BLK, 2 * HD
        )
        result, dquery, terms = sparse_call(
            query_heads, grad_heads, keyvals, allowed.astype(jnp.float32)[:, :, None, :], factor
        )
        terms = terms.reshape(group, H, SLOTS, BLK, 2 * HD)
        spacing = ((0, 0), (0, 0), (0, 0), (0, 0))
        window_sum = (
            jnp.pad(terms[:, :, 0], ((0, 2),) + spacing[1:])
            + jnp.pad(terms[:, :, 1], ((1, 1),) + spacing[1:])
            + jnp.pad(terms[:, :, 2], ((2, 0),) + spacing[1:])
        )
        global_sum = jnp.sum(terms[:, :, 3 : 3 + NG], axis=0)
        random_out = terms[:, :, 3 + NG :].astype(jnp.bfloat16)
        return (result, dquery, window_sum, global_sum, random_out)

    if groups == 1:
        mapped = tuple(part[None] for part in run_group(0))
    else:
        mapped = lax.map(run_group, jnp.arange(groups, dtype=jnp.int32))
    result = mapped[0].reshape(per_dev, H, BLK, HD)
    dquery = mapped[1].reshape(per_dev, H, BLK, HD)
    place = (
        jnp.arange(groups, dtype=jnp.int32)[:, None] * group
        + jnp.arange(group + 2, dtype=jnp.int32)[None, :]
    ).reshape(-1)
    if groups == 1:
        padded_grads = mapped[2].reshape(per_dev + 2, H, BLK, 2 * HD)
    else:
        padded_grads = (
            jnp.zeros((per_dev + 2, H, BLK, 2 * HD), jnp.float32)
            .at[place]
            .add(mapped[2].reshape(-1, H, BLK, 2 * HD))
        )
    global_part = jnp.sum(mapped[3], axis=0).transpose(1, 0, 2, 3)
    random_out = mapped[4].reshape(-1, BLK, 2 * HD)
    own_grads = padded_grads[1 : per_dev + 1]
    edge_pair = jnp.stack([padded_grads[0], padded_grads[per_dev + 1]])
    near_grads = padded_2(edge_pair.astype(jnp.bfloat16), (("seq", 0),), 1).astype(edge_pair.dtype)
    own_grads = own_grads.at[0].add(near_grads[0]).at[per_dev - 1].add(near_grads[3])
    back_buffer = jnp.einsum(
        "se,ef->sf",
        slot_hit.astype(jnp.bfloat16),
        random_out.reshape(-1, BLK * 2 * HD),
        preferred_element_type=jnp.bfloat16,
    ).reshape(devices, capacity, BLK, 2 * HD)
    returned = lax.all_to_all(back_buffer, "seq", split_axis=0, concat_axis=0, tiled=True)
    code_hit = (
        wanted.reshape(-1)[:, None] == jnp.arange(per_dev * H, dtype=jnp.int32)[None, :]
    ).astype(jnp.bfloat16)
    table_grads = jnp.einsum(
        "sc,sf->cf",
        code_hit,
        returned.reshape(-1, BLK * 2 * HD),
        preferred_element_type=jnp.float32,
    ).reshape(per_dev * H, BLK, 2 * HD)
    own_grads = own_grads + table_grads.reshape(per_dev, H, BLK, 2 * HD)
    key_tok = keys.reshape(tokens, H, HD)
    value_tok = values.reshape(tokens, H, HD)
    scores = (
        jnp.einsum("gqhd,khd->ghqk", g_query, key_tok, preferred_element_type=jnp.float32) * factor
    )
    local_max = jnp.max(scores, axis=-1)
    local_expo = jnp.exp(scores - local_max[..., None])
    part_acc = jnp.einsum(
        "ghqk,khd->ghqd",
        local_expo.astype(jnp.bfloat16),
        value_tok,
        preferred_element_type=jnp.float32,
    )
    row_shape = local_max.shape
    packed = jnp.concatenate(
        [local_max[..., None], jnp.sum(local_expo, axis=-1)[..., None], part_acc], axis=-1
    ).reshape(devices, -1, HD + 2)
    got = lax.all_to_all(packed, "seq", 0, 0, tiled=True)
    top = jnp.max(got[..., 0], axis=0)
    scale = jnp.exp(got[..., 0] - top[None])
    tot = jnp.sum(scale * got[..., 1], axis=0)
    acc = jnp.sum(scale[..., None] * got[..., 2:], axis=0) / tot[:, None]
    merged = lax.all_gather(
        jnp.concatenate([top[:, None], tot[:, None], acc], axis=-1), "seq", axis=0, tiled=True
    )
    row_top = merged[:, 0].reshape(row_shape)
    row_tot = merged[:, 1].reshape(row_shape)
    global_out = merged[:, 2:].reshape(row_shape + (HD,))
    probs = jnp.exp(scores - row_top[..., None]) / row_tot[..., None]
    dprobs = jnp.einsum("gqhd,khd->ghqk", g_grad, value_tok, preferred_element_type=jnp.float32)
    dotted = jnp.sum(g_grad.transpose(0, 2, 1, 3).astype(jnp.float32) * global_out, axis=-1)
    dscore = (probs * (dprobs - dotted[..., None])).astype(jnp.bfloat16)
    g_dquery = factor * jnp.einsum(
        "ghqk,khd->ghqd", dscore, key_tok, preferred_element_type=jnp.float32
    )
    tok_dkey = factor * jnp.einsum(
        "ghqk,gqhd->khd", dscore, g_query, preferred_element_type=jnp.float32
    )
    tok_dvalue = jnp.einsum(
        "ghqk,gqhd->khd", probs.astype(jnp.bfloat16), g_grad, preferred_element_type=jnp.float32
    )
    both_sum = summed_to_all(jnp.concatenate([g_dquery, global_part], axis=-1))
    dquery_sum = both_sum[..., :HD]
    global_sum = both_sum[..., HD:]
    for number in range(NG):
        owned = global_blocks[number] // per_dev == me_index
        local_block = global_blocks[number] % per_dev
        result = result.at[local_block].set(
            jnp.where(owned, global_out[number], result[local_block])
        )
        dquery = dquery.at[local_block].add(jnp.where(owned, dquery_sum[number], 0.0))
        own_grads = own_grads.at[local_block].add(jnp.where(owned, global_sum[number], 0.0))
    attended = token_rows(result).astype(jnp.bfloat16)
    query_grad = token_rows(dquery).astype(jnp.bfloat16)
    key_grad = (token_rows(own_grads[..., :HD]) + tok_dkey.reshape(tokens, width)).astype(
        jnp.bfloat16
    )
    value_grad = (token_rows(own_grads[..., HD:]) + tok_dvalue.reshape(tokens, width)).astype(
        jnp.bfloat16
    )
    return (attended, query_grad, key_grad, value_grad)


def solution(mesh):
    return jax.shard_map(
        per_device,
        mesh=mesh,
        in_specs=(
            P(("grp", "seq"), None),
            P(("grp", "seq"), None),
            P(("grp", "seq"), None),
            P(("grp", "seq"), None),
            P(("grp", "seq"), None, None),
            P("grp"),
        ),
        out_specs=(
            P(("grp", "seq"), None),
            P(("grp", "seq"), None),
            P(("grp", "seq"), None),
            P(("grp", "seq"), None),
        ),
        check_vma=False,
    )
```

```python
import math

import jax
import jax.numpy as jnp
from jax import lax
from jax.experimental import pallas as pl
from jax.sharding import PartitionSpec as P

H = 12
HD = 64
BLK = 64
R = 3
NG = 2
QGROUP = 8
SLOTS = 8


def padded_2(block, sides, width):
    for axis, dim in sides:
        count = lax.axis_size(axis)
        forward = [(i, i + 1) for i in range(count - 1)]
        forward.append((count - 1, 0))
        backward = [(target, source) for source, target in forward]
        low = lax.ppermute(
            lax.slice_in_dim(block, block.shape[dim] - width, None, axis=dim), axis, forward
        )
        high = lax.ppermute(lax.slice_in_dim(block, 0, width, axis=dim), axis, backward)
        block = jnp.concatenate([low, block, high], axis=dim)
    return block


def from_owners(value, owners, extra):
    devices = lax.axis_size("seq")
    count = value.shape[0]
    chunks = value.reshape(count, devices, -1).transpose(1, 0, 2).reshape(devices, -1)
    width = chunks.shape[1]
    packed = jnp.concatenate([chunks, extra.astype(value.dtype)], axis=1)
    got = lax.all_to_all(packed, "seq", 0, 0, tiled=True)
    rows = got[:, :width].reshape(devices, count, -1)
    mine = jnp.stack([rows[owners[i], i] for i in range(count)])
    full = lax.all_gather(mine, "seq", axis=0, tiled=False)
    return full.transpose(1, 0, 2).reshape(value.shape), got[:, width:].astype(extra.dtype)


def summed_to_all(value):
    devices = lax.axis_size("seq")
    chunks = value.astype(jnp.bfloat16).reshape(devices, -1)
    got = lax.all_to_all(chunks, "seq", 0, 0, tiled=True)
    total = jnp.sum(got.astype(jnp.float32), axis=0).astype(jnp.bfloat16)
    full = lax.all_gather(total, "seq", axis=0, tiled=True)
    return full.reshape(value.shape).astype(jnp.float32)


def head_blocks(matrix, blocks):
    return matrix.reshape(blocks, BLK, H, HD).transpose(0, 2, 1, 3)


def token_rows(blocked):
    blocks = blocked.shape[0]
    return blocked.transpose(0, 2, 1, 3).reshape(blocks * BLK, H * HD)


def pair_heads(rows, blocks):
    return (
        rows.reshape(blocks, BLK, 2, H, HD).transpose(0, 3, 1, 2, 4).reshape(blocks, H, BLK, 2 * HD)
    )


def slot_plan(block_lists, per_dev, devices, head_ids):
    owners = (block_lists // per_dev).reshape(-1)
    req_codes = (block_lists % per_dev * H + head_ids[None, :, None]).reshape(-1)
    onehot = (owners[:, None] == jnp.arange(devices, dtype=jnp.int32)[None, :]).astype(jnp.int32)
    before = jnp.cumsum(onehot, axis=0) - onehot
    return (owners, jnp.sum(before * onehot, axis=1), req_codes)


def sparse_group(query_g, grad_g, keyvals, allowed, factor):
    key_part = keyvals[..., :HD]
    value_part = keyvals[..., HD:]
    scores = (
        jnp.einsum("ghqd,ghkd->ghqk", query_g, key_part, preferred_element_type=jnp.float32)
        * factor
    )
    mask = allowed[:, :, None, :]
    row_max = jnp.max(jnp.where(mask, scores, -1e30), axis=-1, keepdims=True)
    expo = jnp.where(mask, jnp.exp(scores - row_max), 0.0)
    totals = jnp.sum(expo, axis=-1, keepdims=True)
    result = (
        jnp.einsum(
            "ghqk,ghkd->ghqd",
            expo.astype(jnp.bfloat16),
            value_part,
            preferred_element_type=jnp.float32,
        )
        / totals
    )
    probs = expo / totals
    dprobs = jnp.einsum("ghqd,ghkd->ghqk", grad_g, value_part, preferred_element_type=jnp.float32)
    dotted = jnp.sum(grad_g.astype(jnp.float32) * result, axis=-1, keepdims=True)
    dscore = (probs * (dprobs - dotted)).astype(jnp.bfloat16)
    dquery = factor * jnp.einsum(
        "ghqk,ghkd->ghqd", dscore, key_part, preferred_element_type=jnp.float32
    )
    dkey = factor * jnp.einsum(
        "ghqk,ghqd->ghkd", dscore, query_g, preferred_element_type=jnp.float32
    )
    dvalue = jnp.einsum(
        "ghqk,ghqd->ghkd", probs.astype(jnp.bfloat16), grad_g, preferred_element_type=jnp.float32
    )
    stats = jnp.stack([row_max[..., 0], totals[..., 0], dotted[..., 0]], axis=1)
    return (result, dquery, jnp.concatenate([dkey, dvalue], axis=-1), stats)


def sparse_kernel(q_ref, g_ref, kv_ref, allow_ref, out_ref, dq_ref, terms_ref, *, factor):
    nt = (((1,), (1,)), ((), ()))
    for head in range(q_ref.shape[1]):
        query = q_ref[0, head]
        grad = g_ref[0, head]
        keyval = kv_ref[0, head]
        key = keyval[:, :HD]
        value = keyval[:, HD:]
        scores = lax.dot_general(query, key, nt, preferred_element_type=jnp.float32) * factor
        mask = allow_ref[0, head] > 0.5
        row_max = jnp.max(jnp.where(mask, scores, -1e30), axis=-1, keepdims=True)
        expo = jnp.where(mask, jnp.exp(scores - row_max), 0.0)
        totals = jnp.sum(expo, axis=-1, keepdims=True)
        result = (
            jnp.dot(expo.astype(jnp.bfloat16), value, preferred_element_type=jnp.float32)
            / totals
        )
        probs = expo / totals
        dprobs = lax.dot_general(grad, value, nt, preferred_element_type=jnp.float32)
        dotted = jnp.sum(grad.astype(jnp.float32) * result, axis=-1, keepdims=True)
        dscore = probs * (dprobs - dotted)
        dq = factor * jnp.dot(dscore.astype(jnp.bfloat16), key, preferred_element_type=jnp.float32)
        dkey = factor * jnp.dot(
            dscore.T.astype(jnp.bfloat16), query, preferred_element_type=jnp.float32
        )
        dvalue = jnp.dot(probs.T.astype(jnp.bfloat16), grad, preferred_element_type=jnp.float32)
        out_ref[0, head] = result
        dq_ref[0, head] = dq
        terms_ref[0, head, :, :HD] = dkey
        terms_ref[0, head, :, HD:] = dvalue


def sparse_call(query_h, grad_h, keyvals, allowed_f, factor, interpret=False, per_step=4):
    blocks, heads, rows, _ = query_h.shape
    keys_n = keyvals.shape[2]
    small = pl.BlockSpec((1, per_step, rows, HD), lambda i, h: (i, h, 0, 0))
    return pl.pallas_call(
        lambda *refs: sparse_kernel(*refs, factor=factor),
        grid=(blocks, heads // per_step),
        in_specs=[
            small,
            small,
            pl.BlockSpec((1, per_step, keys_n, 2 * HD), lambda i, h: (i, h, 0, 0)),
            pl.BlockSpec((1, per_step, 1, keys_n), lambda i, h: (i, h, 0, 0)),
        ],
        out_specs=[
            small,
            small,
            pl.BlockSpec((1, per_step, keys_n, 2 * HD), lambda i, h: (i, h, 0, 0)),
        ],
        out_shape=[
            jax.ShapeDtypeStruct((blocks, heads, rows, HD), jnp.float32),
            jax.ShapeDtypeStruct((blocks, heads, rows, HD), jnp.float32),
            jax.ShapeDtypeStruct((blocks, heads, keys_n, 2 * HD), jnp.float32),
        ],
        interpret=interpret,
    )(query_h, grad_h, keyvals, allowed_f)


def per_device(queries, keys, values, out_grad, random_blocks, global_blocks):
    tokens = queries.shape[0]
    width = queries.shape[1]
    per_dev = tokens // BLK
    devices = lax.axis_size("seq")
    me_index = lax.axis_index("seq")
    blocks_all = per_dev * devices
    factor = 1.0 / math.sqrt(HD)
    entry_count = per_dev * H * R
    capacity = (entry_count + devices - 2) // (devices - 1) + 4
    head_ids = jnp.arange(H, dtype=jnp.int32)
    block_ids = me_index * per_dev + jnp.arange(per_dev, dtype=jnp.int32)
    is_global = jnp.any(block_ids[:, None] == global_blocks[None, :], axis=1)
    row_global = jnp.repeat(is_global, BLK)
    masked = jnp.where(row_global[:, None], jnp.zeros_like(out_grad), out_grad)
    kv_rows = jnp.concatenate([keys, values], axis=1)
    edge_rows = jnp.concatenate([kv_rows[:BLK], kv_rows[-BLK:]], axis=0)
    padded = padded_2(edge_rows, (("seq", 0),), BLK)
    left_rows = padded[:BLK]
    right_rows = padded[3 * BLK :]
    extended = jnp.concatenate(
        [
            left_rows[None, :, : 2 * width],
            kv_rows.reshape(per_dev, BLK, 2 * width),
            right_rows[None, :, : 2 * width],
        ],
        axis=0,
    )
    kv_heads = pair_heads(extended, per_dev + 2)
    kv_local = kv_heads[1 : per_dev + 1]
    global_rows = []
    for number in range(NG):
        row_start = global_blocks[number] % per_dev * BLK
        global_rows.append(
            jnp.concatenate(
                [
                    lax.dynamic_slice_in_dim(source, row_start, BLK, 0)
                    for source in (queries, keys, values, out_grad)
                ],
                axis=1,
            )
        )
    stacked_rows = jnp.stack(global_rows)
    owners, slot_ids, req_codes = slot_plan(random_blocks, per_dev, devices, head_ids)
    slot_key = owners * capacity + slot_ids
    slot_hit = jnp.arange(devices * capacity, dtype=jnp.int32)[:, None] == slot_key[None, :]
    outgoing = jnp.where(
        jnp.any(slot_hit, axis=1), jnp.sum(jnp.where(slot_hit, req_codes[None, :], 0), axis=1), -1
    ).reshape(devices, capacity)
    grows, wanted = from_owners(stacked_rows, global_blocks // per_dev, outgoing)
    sending = kv_local.reshape(per_dev * H, BLK, 2 * HD)[jnp.maximum(wanted, 0)]
    g_query = grows[:, :, :width].reshape(NG, BLK, H, HD)
    g_grad = grows[:, :, 3 * width :].reshape(NG, BLK, H, HD)
    g_kv = pair_heads(grows[:, :, width : 3 * width], NG)
    fetched = lax.all_to_all(sending, "seq", split_axis=0, concat_axis=0, tiled=True)
    rand_kv = fetched[owners, slot_ids].reshape(per_dev, H, R, BLK, 2 * HD)
    shifts = jnp.arange(-1, 2, dtype=jnp.int32)
    window_ids = (block_ids[:, None] + shifts[None, :]) % blocks_all
    other_ids = jnp.concatenate(
        [jnp.broadcast_to(window_ids[:, None, :], (per_dev, H, 3)), random_blocks], axis=2
    )
    global_kept = jnp.all(global_blocks[None, None, :, None] != other_ids[:, :, None, :], axis=3)
    allowed = jnp.concatenate(
        [jnp.ones((per_dev, H, 3), jnp.bool_), global_kept, jnp.ones((per_dev, H, R), jnp.bool_)],
        axis=2,
    )
    allowed = jnp.repeat(allowed, BLK, axis=2)
    query_heads = head_blocks(queries, per_dev)
    grad_heads = head_blocks(masked, per_dev)
    group = QGROUP
    groups = per_dev // group
    glob_slots = jnp.broadcast_to(g_kv.transpose(1, 0, 2, 3)[None], (group, H, NG, BLK, 2 * HD))

    def run_group(number):
        win_slots = jnp.stack(
            [kv_heads[0:group], kv_heads[1 : group + 1], kv_heads[2 : group + 2]], axis=2
        )
        keyvals = jnp.concatenate([win_slots, glob_slots, rand_kv], axis=2).reshape(
            group, H, SLOTS * BLK, 2 * HD
        )
        result, dquery, terms = sparse_call(
            query_heads, grad_heads, keyvals, allowed.astype(jnp.float32)[:, :, None, :], factor
        )
        terms = terms.reshape(group, H, SLOTS, BLK, 2 * HD)
        spacing = ((0, 0), (0, 0), (0, 0), (0, 0))
        window_sum = (
            jnp.pad(terms[:, :, 0], ((0, 2),) + spacing[1:])
            + jnp.pad(terms[:, :, 1], ((1, 1),) + spacing[1:])
            + jnp.pad(terms[:, :, 2], ((2, 0),) + spacing[1:])
        )
        global_sum = jnp.sum(terms[:, :, 3 : 3 + NG], axis=0)
        random_out = terms[:, :, 3 + NG :].astype(jnp.bfloat16)
        return (result, dquery, window_sum, global_sum, random_out)

    if groups == 1:
        mapped = tuple(part[None] for part in run_group(0))
    else:
        mapped = lax.map(run_group, jnp.arange(groups, dtype=jnp.int32))
    result = mapped[0].reshape(per_dev, H, BLK, HD)
    dquery = mapped[1].reshape(per_dev, H, BLK, HD)
    place = (
        jnp.arange(groups, dtype=jnp.int32)[:, None] * group
        + jnp.arange(group + 2, dtype=jnp.int32)[None, :]
    ).reshape(-1)
    if groups == 1:
        padded_grads = mapped[2].reshape(per_dev + 2, H, BLK, 2 * HD)
    else:
        padded_grads = (
            jnp.zeros((per_dev + 2, H, BLK, 2 * HD), jnp.float32)
            .at[place]
            .add(mapped[2].reshape(-1, H, BLK, 2 * HD))
        )
    global_part = jnp.sum(mapped[3], axis=0).transpose(1, 0, 2, 3)
    random_out = mapped[4].reshape(-1, BLK, 2 * HD)
    own_grads = padded_grads[1 : per_dev + 1]
    edge_pair = jnp.stack([padded_grads[0], padded_grads[per_dev + 1]])
    near_grads = padded_2(edge_pair.astype(jnp.bfloat16), (("seq", 0),), 1).astype(edge_pair.dtype)
    own_grads = own_grads.at[0].add(near_grads[0]).at[per_dev - 1].add(near_grads[3])
    back_buffer = jnp.einsum(
        "se,ef->sf",
        slot_hit.astype(jnp.bfloat16),
        random_out.reshape(-1, BLK * 2 * HD),
        preferred_element_type=jnp.bfloat16,
    ).reshape(devices, capacity, BLK, 2 * HD)
    returned = lax.all_to_all(back_buffer, "seq", split_axis=0, concat_axis=0, tiled=True)
    code_hit = (
        wanted.reshape(-1)[:, None] == jnp.arange(per_dev * H, dtype=jnp.int32)[None, :]
    ).astype(jnp.bfloat16)
    table_grads = jnp.einsum(
        "sc,sf->cf",
        code_hit,
        returned.reshape(-1, BLK * 2 * HD),
        preferred_element_type=jnp.float32,
    ).reshape(per_dev * H, BLK, 2 * HD)
    own_grads = own_grads + table_grads.reshape(per_dev, H, BLK, 2 * HD)
    key_tok = keys.reshape(tokens, H, HD)
    value_tok = values.reshape(tokens, H, HD)
    scores = (
        jnp.einsum("gqhd,khd->ghqk", g_query, key_tok, preferred_element_type=jnp.float32) * factor
    )
    local_max = jnp.max(scores, axis=-1)
    local_expo = jnp.exp(scores - local_max[..., None])
    part_acc = jnp.einsum(
        "ghqk,khd->ghqd",
        local_expo.astype(jnp.bfloat16),
        value_tok,
        preferred_element_type=jnp.float32,
    )
    row_shape = local_max.shape
    packed = jnp.concatenate(
        [local_max[..., None], jnp.sum(local_expo, axis=-1)[..., None], part_acc], axis=-1
    ).reshape(devices, -1, HD + 2)
    got = lax.all_to_all(packed, "seq", 0, 0, tiled=True)
    top = jnp.max(got[..., 0], axis=0)
    scale = jnp.exp(got[..., 0] - top[None])
    tot = jnp.sum(scale * got[..., 1], axis=0)
    acc = jnp.sum(scale[..., None] * got[..., 2:], axis=0) / tot[:, None]
    merged = lax.all_gather(
        jnp.concatenate([top[:, None], tot[:, None], acc], axis=-1), "seq", axis=0, tiled=True
    )
    row_top = merged[:, 0].reshape(row_shape)
    row_tot = merged[:, 1].reshape(row_shape)
    global_out = merged[:, 2:].reshape(row_shape + (HD,))
    probs = jnp.exp(scores - row_top[..., None]) / row_tot[..., None]
    dprobs = jnp.einsum("gqhd,khd->ghqk", g_grad, value_tok, preferred_element_type=jnp.float32)
    dotted = jnp.sum(g_grad.transpose(0, 2, 1, 3).astype(jnp.float32) * global_out, axis=-1)
    dscore = (probs * (dprobs - dotted[..., None])).astype(jnp.bfloat16)
    g_dquery = factor * jnp.einsum(
        "ghqk,khd->ghqd", dscore, key_tok, preferred_element_type=jnp.float32
    )
    tok_dkey = factor * jnp.einsum(
        "ghqk,gqhd->khd", dscore, g_query, preferred_element_type=jnp.float32
    )
    tok_dvalue = jnp.einsum(
        "ghqk,gqhd->khd", probs.astype(jnp.bfloat16), g_grad, preferred_element_type=jnp.float32
    )
    both_sum = summed_to_all(jnp.concatenate([g_dquery, global_part], axis=-1))
    dquery_sum = both_sum[..., :HD]
    global_sum = both_sum[..., HD:]
    for number in range(NG):
        owned = global_blocks[number] // per_dev == me_index
        local_block = global_blocks[number] % per_dev
        result = result.at[local_block].set(
            jnp.where(owned, global_out[number], result[local_block])
        )
        dquery = dquery.at[local_block].add(jnp.where(owned, dquery_sum[number], 0.0))
        own_grads = own_grads.at[local_block].add(jnp.where(owned, global_sum[number], 0.0))
    attended = token_rows(result).astype(jnp.bfloat16)
    query_grad = token_rows(dquery).astype(jnp.bfloat16)
    key_grad = (token_rows(own_grads[..., :HD]) + tok_dkey.reshape(tokens, width)).astype(
        jnp.bfloat16
    )
    value_grad = (token_rows(own_grads[..., HD:]) + tok_dvalue.reshape(tokens, width)).astype(
        jnp.bfloat16
    )
    return (attended, query_grad, key_grad, value_grad)


def solution(mesh):
    return jax.shard_map(
        per_device,
        mesh=mesh,
        in_specs=(
            P(("grp", "seq"), None),
            P(("grp", "seq"), None),
            P(("grp", "seq"), None),
            P(("grp", "seq"), None),
            P(("grp", "seq"), None, None),
            P("grp"),
        ),
        out_specs=(
            P(("grp", "seq"), None),
            P(("grp", "seq"), None),
            P(("grp", "seq"), None),
            P(("grp", "seq"), None),
        ),
        check_vma=False,
    )
```

```python
import math

import jax
import jax.numpy as jnp
from jax import lax
from jax.experimental import pallas as pl
from jax.sharding import PartitionSpec as P

H = 12
HD = 64
BLK = 64
R = 3
NG = 2
QGROUP = 8
SLOTS = 8


def padded_2(block, sides, width):
    for axis, dim in sides:
        count = lax.axis_size(axis)
        forward = [(i, i + 1) for i in range(count - 1)]
        forward.append((count - 1, 0))
        backward = [(target, source) for source, target in forward]
        low = lax.ppermute(
            lax.slice_in_dim(block, block.shape[dim] - width, None, axis=dim), axis, forward
        )
        high = lax.ppermute(lax.slice_in_dim(block, 0, width, axis=dim), axis, backward)
        block = jnp.concatenate([low, block, high], axis=dim)
    return block


def from_owners(value, owners, extra):
    devices = lax.axis_size("seq")
    count = value.shape[0]
    chunks = value.reshape(count, devices, -1).transpose(1, 0, 2).reshape(devices, -1)
    width = chunks.shape[1]
    packed = jnp.concatenate([chunks, extra.astype(value.dtype)], axis=1)
    got = lax.all_to_all(packed, "seq", 0, 0, tiled=True)
    rows = got[:, :width].reshape(devices, count, -1)
    mine = jnp.stack([rows[owners[i], i] for i in range(count)])
    full = lax.all_gather(mine, "seq", axis=0, tiled=False)
    return full.transpose(1, 0, 2).reshape(value.shape), got[:, width:].astype(extra.dtype)


def summed_to_all(value):
    devices = lax.axis_size("seq")
    chunks = value.astype(jnp.bfloat16).reshape(devices, -1)
    got = lax.all_to_all(chunks, "seq", 0, 0, tiled=True)
    total = jnp.sum(got.astype(jnp.float32), axis=0).astype(jnp.bfloat16)
    full = lax.all_gather(total, "seq", axis=0, tiled=True)
    return full.reshape(value.shape).astype(jnp.float32)


def head_blocks(matrix, blocks):
    return matrix.reshape(blocks, BLK, H, HD).transpose(0, 2, 1, 3)


def token_rows(blocked):
    blocks = blocked.shape[0]
    return blocked.transpose(0, 2, 1, 3).reshape(blocks * BLK, H * HD)


def pair_heads(rows, blocks):
    return (
        rows.reshape(blocks, BLK, 2, H, HD).transpose(0, 3, 1, 2, 4).reshape(blocks, H, BLK, 2 * HD)
    )


def slot_plan(block_lists, per_dev, devices, head_ids):
    owners = (block_lists // per_dev).reshape(-1)
    req_codes = (block_lists % per_dev * H + head_ids[None, :, None]).reshape(-1)
    onehot = (owners[:, None] == jnp.arange(devices, dtype=jnp.int32)[None, :]).astype(jnp.int32)
    before = jnp.cumsum(onehot, axis=0) - onehot
    return (owners, jnp.sum(before * onehot, axis=1), req_codes)


def sparse_group(query_g, grad_g, keyvals, allowed, factor):
    key_part = keyvals[..., :HD]
    value_part = keyvals[..., HD:]
    scores = (
        jnp.einsum("ghqd,ghkd->ghqk", query_g, key_part, preferred_element_type=jnp.float32)
        * factor
    )
    mask = allowed[:, :, None, :]
    row_max = jnp.max(jnp.where(mask, scores, -1e30), axis=-1, keepdims=True)
    expo = jnp.where(mask, jnp.exp(scores - row_max), 0.0)
    totals = jnp.sum(expo, axis=-1, keepdims=True)
    result = (
        jnp.einsum(
            "ghqk,ghkd->ghqd",
            expo.astype(jnp.bfloat16),
            value_part,
            preferred_element_type=jnp.float32,
        )
        / totals
    )
    probs = expo / totals
    dprobs = jnp.einsum("ghqd,ghkd->ghqk", grad_g, value_part, preferred_element_type=jnp.float32)
    dotted = jnp.sum(grad_g.astype(jnp.float32) * result, axis=-1, keepdims=True)
    dscore = (probs * (dprobs - dotted)).astype(jnp.bfloat16)
    dquery = factor * jnp.einsum(
        "ghqk,ghkd->ghqd", dscore, key_part, preferred_element_type=jnp.float32
    )
    dkey = factor * jnp.einsum(
        "ghqk,ghqd->ghkd", dscore, query_g, preferred_element_type=jnp.float32
    )
    dvalue = jnp.einsum(
        "ghqk,ghqd->ghkd", probs.astype(jnp.bfloat16), grad_g, preferred_element_type=jnp.float32
    )
    stats = jnp.stack([row_max[..., 0], totals[..., 0], dotted[..., 0]], axis=1)
    return (result, dquery, jnp.concatenate([dkey, dvalue], axis=-1), stats)


def sparse_kernel(q_ref, g_ref, kv_ref, allow_ref, out_ref, dq_ref, terms_ref, *, factor):
    nt = (((1,), (1,)), ((), ()))
    for head in range(q_ref.shape[1]):
        query = q_ref[0, head]
        grad = g_ref[0, head]
        keyval = kv_ref[0, head]
        key = keyval[:, :HD]
        value = keyval[:, HD:]
        scores = lax.dot_general(query, key, nt, preferred_element_type=jnp.float32) * factor
        mask = allow_ref[0, head] > 0.5
        row_max = jnp.max(jnp.where(mask, scores, -1e30), axis=-1, keepdims=True)
        expo = jnp.where(mask, jnp.exp(scores - row_max), 0.0)
        totals = jnp.sum(expo, axis=-1, keepdims=True)
        result = (
            jnp.dot(expo.astype(jnp.bfloat16), value, preferred_element_type=jnp.float32)
            / totals
        )
        probs = expo / totals
        dprobs = lax.dot_general(grad, value, nt, preferred_element_type=jnp.float32)
        dotted = jnp.sum(grad.astype(jnp.float32) * result, axis=-1, keepdims=True)
        dscore = probs * (dprobs - dotted)
        dq = factor * jnp.dot(dscore.astype(jnp.bfloat16), key, preferred_element_type=jnp.float32)
        dkey = factor * jnp.dot(
            dscore.T.astype(jnp.bfloat16), query, preferred_element_type=jnp.float32
        )
        dvalue = jnp.dot(probs.T.astype(jnp.bfloat16), grad, preferred_element_type=jnp.float32)
        out_ref[0, head] = result
        dq_ref[0, head] = dq
        terms_ref[0, head, :, :HD] = dkey
        terms_ref[0, head, :, HD:] = dvalue


def sparse_call(query_h, grad_h, keyvals, allowed_f, factor, interpret=False, per_step=4):
    blocks, heads, rows, _ = query_h.shape
    keys_n = keyvals.shape[2]
    small = pl.BlockSpec((1, per_step, rows, HD), lambda i, h: (i, h, 0, 0))
    return pl.pallas_call(
        lambda *refs: sparse_kernel(*refs, factor=factor),
        grid=(blocks, heads // per_step),
        in_specs=[
            small,
            small,
            pl.BlockSpec((1, per_step, keys_n, 2 * HD), lambda i, h: (i, h, 0, 0)),
            pl.BlockSpec((1, per_step, 1, keys_n), lambda i, h: (i, h, 0, 0)),
        ],
        out_specs=[
            small,
            small,
            pl.BlockSpec((1, per_step, keys_n, 2 * HD), lambda i, h: (i, h, 0, 0)),
        ],
        out_shape=[
            jax.ShapeDtypeStruct((blocks, heads, rows, HD), jnp.float32),
            jax.ShapeDtypeStruct((blocks, heads, rows, HD), jnp.float32),
            jax.ShapeDtypeStruct((blocks, heads, keys_n, 2 * HD), jnp.float32),
        ],
        interpret=interpret,
    )(query_h, grad_h, keyvals, allowed_f)


def per_device(queries, keys, values, out_grad, random_blocks, global_blocks):
    tokens = queries.shape[0]
    width = queries.shape[1]
    per_dev = tokens // BLK
    devices = lax.axis_size("seq")
    me_index = lax.axis_index("seq")
    blocks_all = per_dev * devices
    factor = 1.0 / math.sqrt(HD)
    entry_count = per_dev * H * R
    capacity = (entry_count + devices - 2) // (devices - 1) + 4
    head_ids = jnp.arange(H, dtype=jnp.int32)
    block_ids = me_index * per_dev + jnp.arange(per_dev, dtype=jnp.int32)
    is_global = jnp.any(block_ids[:, None] == global_blocks[None, :], axis=1)
    row_global = jnp.repeat(is_global, BLK)
    masked = jnp.where(row_global[:, None], jnp.zeros_like(out_grad), out_grad)
    kv_rows = jnp.concatenate([keys, values], axis=1)
    edge_rows = jnp.concatenate([kv_rows[:BLK], kv_rows[-BLK:]], axis=0)
    padded = padded_2(edge_rows, (("seq", 0),), BLK)
    left_rows = padded[:BLK]
    right_rows = padded[3 * BLK :]
    extended = jnp.concatenate(
        [
            left_rows[None, :, : 2 * width],
            kv_rows.reshape(per_dev, BLK, 2 * width),
            right_rows[None, :, : 2 * width],
        ],
        axis=0,
    )
    kv_heads = pair_heads(extended, per_dev + 2)
    kv_local = kv_heads[1 : per_dev + 1]
    global_rows = []
    for number in range(NG):
        row_start = global_blocks[number] % per_dev * BLK
        global_rows.append(
            jnp.concatenate(
                [
                    lax.dynamic_slice_in_dim(source, row_start, BLK, 0)
                    for source in (queries, keys, values, out_grad)
                ],
                axis=1,
            )
        )
    stacked_rows = jnp.stack(global_rows)
    owners, slot_ids, req_codes = slot_plan(random_blocks, per_dev, devices, head_ids)
    slot_key = owners * capacity + slot_ids
    slot_hit = jnp.arange(devices * capacity, dtype=jnp.int32)[:, None] == slot_key[None, :]
    outgoing = jnp.where(
        jnp.any(slot_hit, axis=1), jnp.sum(jnp.where(slot_hit, req_codes[None, :], 0), axis=1), -1
    ).reshape(devices, capacity)
    grows, wanted = from_owners(stacked_rows, global_blocks // per_dev, outgoing)
    sending = kv_local.reshape(per_dev * H, BLK, 2 * HD)[jnp.maximum(wanted, 0)]
    g_query = grows[:, :, :width].reshape(NG, BLK, H, HD)
    g_grad = grows[:, :, 3 * width :].reshape(NG, BLK, H, HD)
    g_kv = pair_heads(grows[:, :, width : 3 * width], NG)
    fetched = lax.all_to_all(sending, "seq", split_axis=0, concat_axis=0, tiled=True)
    rand_kv = fetched[owners, slot_ids].reshape(per_dev, H, R, BLK, 2 * HD)
    shifts = jnp.arange(-1, 2, dtype=jnp.int32)
    window_ids = (block_ids[:, None] + shifts[None, :]) % blocks_all
    other_ids = jnp.concatenate(
        [jnp.broadcast_to(window_ids[:, None, :], (per_dev, H, 3)), random_blocks], axis=2
    )
    global_kept = jnp.all(global_blocks[None, None, :, None] != other_ids[:, :, None, :], axis=3)
    allowed = jnp.concatenate(
        [jnp.ones((per_dev, H, 3), jnp.bool_), global_kept, jnp.ones((per_dev, H, R), jnp.bool_)],
        axis=2,
    )
    allowed = jnp.repeat(allowed, BLK, axis=2)
    query_heads = head_blocks(queries, per_dev)
    grad_heads = head_blocks(masked, per_dev)
    group = QGROUP
    groups = per_dev // group
    glob_slots = jnp.broadcast_to(g_kv.transpose(1, 0, 2, 3)[None], (group, H, NG, BLK, 2 * HD))

    def run_group(number):
        win_slots = jnp.stack(
            [kv_heads[0:group], kv_heads[1 : group + 1], kv_heads[2 : group + 2]], axis=2
        )
        keyvals = jnp.concatenate([win_slots, glob_slots, rand_kv], axis=2).reshape(
            group, H, SLOTS * BLK, 2 * HD
        )
        result, dquery, terms = sparse_call(
            query_heads, grad_heads, keyvals, allowed.astype(jnp.float32)[:, :, None, :], factor
        )
        terms = terms.reshape(group, H, SLOTS, BLK, 2 * HD)
        spacing = ((0, 0), (0, 0), (0, 0), (0, 0))
        window_sum = (
            jnp.pad(terms[:, :, 0], ((0, 2),) + spacing[1:])
            + jnp.pad(terms[:, :, 1], ((1, 1),) + spacing[1:])
            + jnp.pad(terms[:, :, 2], ((2, 0),) + spacing[1:])
        )
        global_sum = jnp.sum(terms[:, :, 3 : 3 + NG], axis=0)
        random_out = terms[:, :, 3 + NG :].astype(jnp.bfloat16)
        return (result, dquery, window_sum, global_sum, random_out)

    if groups == 1:
        mapped = tuple(part[None] for part in run_group(0))
    else:
        mapped = lax.map(run_group, jnp.arange(groups, dtype=jnp.int32))
    result = mapped[0].reshape(per_dev, H, BLK, HD)
    dquery = mapped[1].reshape(per_dev, H, BLK, HD)
    place = (
        jnp.arange(groups, dtype=jnp.int32)[:, None] * group
        + jnp.arange(group + 2, dtype=jnp.int32)[None, :]
    ).reshape(-1)
    if groups == 1:
        padded_grads = mapped[2].reshape(per_dev + 2, H, BLK, 2 * HD)
    else:
        padded_grads = (
            jnp.zeros((per_dev + 2, H, BLK, 2 * HD), jnp.float32)
            .at[place]
            .add(mapped[2].reshape(-1, H, BLK, 2 * HD))
        )
    global_part = jnp.sum(mapped[3], axis=0).transpose(1, 0, 2, 3)
    random_out = mapped[4].reshape(-1, BLK, 2 * HD)
    own_grads = padded_grads[1 : per_dev + 1]
    edge_pair = jnp.stack([padded_grads[0], padded_grads[per_dev + 1]])
    near_grads = padded_2(edge_pair.astype(jnp.bfloat16), (("seq", 0),), 1).astype(edge_pair.dtype)
    own_grads = own_grads.at[0].add(near_grads[0]).at[per_dev - 1].add(near_grads[3])
    back_buffer = jnp.einsum(
        "se,ef->sf",
        slot_hit.astype(jnp.bfloat16),
        random_out.reshape(-1, BLK * 2 * HD),
        preferred_element_type=jnp.bfloat16,
    ).reshape(devices, capacity, BLK, 2 * HD)
    returned = lax.all_to_all(back_buffer, "seq", split_axis=0, concat_axis=0, tiled=True)
    code_hit = (
        wanted.reshape(-1)[:, None] == jnp.arange(per_dev * H, dtype=jnp.int32)[None, :]
    ).astype(jnp.bfloat16)
    table_grads = jnp.einsum(
        "sc,sf->cf",
        code_hit,
        returned.reshape(-1, BLK * 2 * HD),
        preferred_element_type=jnp.float32,
    ).reshape(per_dev * H, BLK, 2 * HD)
    own_grads = own_grads + table_grads.reshape(per_dev, H, BLK, 2 * HD)
    key_tok = keys.reshape(tokens, H, HD)
    value_tok = values.reshape(tokens, H, HD)
    scores = (
        jnp.einsum("gqhd,khd->ghqk", g_query, key_tok, preferred_element_type=jnp.float32) * factor
    )
    local_max = jnp.max(scores, axis=-1)
    local_expo = jnp.exp(scores - local_max[..., None])
    part_acc = jnp.einsum(
        "ghqk,khd->ghqd",
        local_expo.astype(jnp.bfloat16),
        value_tok,
        preferred_element_type=jnp.float32,
    )
    row_shape = local_max.shape
    packed = jnp.concatenate(
        [local_max[..., None], jnp.sum(local_expo, axis=-1)[..., None], part_acc], axis=-1
    ).reshape(devices, -1, HD + 2)
    got = lax.all_to_all(packed, "seq", 0, 0, tiled=True)
    top = jnp.max(got[..., 0], axis=0)
    scale = jnp.exp(got[..., 0] - top[None])
    tot = jnp.sum(scale * got[..., 1], axis=0)
    acc = jnp.sum(scale[..., None] * got[..., 2:], axis=0) / tot[:, None]
    merged = lax.all_gather(
        jnp.concatenate([top[:, None], tot[:, None], acc], axis=-1), "seq", axis=0, tiled=True
    )
    row_top = merged[:, 0].reshape(row_shape)
    row_tot = merged[:, 1].reshape(row_shape)
    global_out = merged[:, 2:].reshape(row_shape + (HD,))
    probs = jnp.exp(scores - row_top[..., None]) / row_tot[..., None]
    dprobs = jnp.einsum("gqhd,khd->ghqk", g_grad, value_tok, preferred_element_type=jnp.float32)
    dotted = jnp.sum(g_grad.transpose(0, 2, 1, 3).astype(jnp.float32) * global_out, axis=-1)
    dscore = (probs * (dprobs - dotted[..., None])).astype(jnp.bfloat16)
    g_dquery = factor * jnp.einsum(
        "ghqk,khd->ghqd", dscore, key_tok, preferred_element_type=jnp.float32
    )
    tok_dkey = factor * jnp.einsum(
        "ghqk,gqhd->khd", dscore, g_query, preferred_element_type=jnp.float32
    )
    tok_dvalue = jnp.einsum(
        "ghqk,gqhd->khd", probs.astype(jnp.bfloat16), g_grad, preferred_element_type=jnp.float32
    )
    both_sum = lax.psum(
        jnp.concatenate([g_dquery, global_part], axis=-1).astype(jnp.bfloat16), "seq"
    ).astype(jnp.float32)
    dquery_sum = both_sum[..., :HD]
    global_sum = both_sum[..., HD:]
    for number in range(NG):
        owned = global_blocks[number] // per_dev == me_index
        local_block = global_blocks[number] % per_dev
        result = result.at[local_block].set(
            jnp.where(owned, global_out[number], result[local_block])
        )
        dquery = dquery.at[local_block].add(jnp.where(owned, dquery_sum[number], 0.0))
        own_grads = own_grads.at[local_block].add(jnp.where(owned, global_sum[number], 0.0))
    attended = token_rows(result).astype(jnp.bfloat16)
    query_grad = token_rows(dquery).astype(jnp.bfloat16)
    key_grad = (token_rows(own_grads[..., :HD]) + tok_dkey.reshape(tokens, width)).astype(
        jnp.bfloat16
    )
    value_grad = (token_rows(own_grads[..., HD:]) + tok_dvalue.reshape(tokens, width)).astype(
        jnp.bfloat16
    )
    return (attended, query_grad, key_grad, value_grad)


def solution(mesh):
    return jax.shard_map(
        per_device,
        mesh=mesh,
        in_specs=(
            P(("grp", "seq"), None),
            P(("grp", "seq"), None),
            P(("grp", "seq"), None),
            P(("grp", "seq"), None),
            P(("grp", "seq"), None, None),
            P("grp"),
        ),
        out_specs=(
            P(("grp", "seq"), None),
            P(("grp", "seq"), None),
            P(("grp", "seq"), None),
            P(("grp", "seq"), None),
        ),
        check_vma=False,
    )
```

```python
import math

import jax
import jax.numpy as jnp
from jax import lax
from jax.experimental import pallas as pl
from jax.sharding import PartitionSpec as P

H = 12
HD = 64
BLK = 64
R = 3
NG = 2
QGROUP = 8
SLOTS = 8


def padded_2(block, sides, width):
    for axis, dim in sides:
        count = lax.axis_size(axis)
        forward = [(i, i + 1) for i in range(count - 1)]
        forward.append((count - 1, 0))
        backward = [(target, source) for source, target in forward]
        low = lax.ppermute(
            lax.slice_in_dim(block, block.shape[dim] - width, None, axis=dim), axis, forward
        )
        high = lax.ppermute(lax.slice_in_dim(block, 0, width, axis=dim), axis, backward)
        block = jnp.concatenate([low, block, high], axis=dim)
    return block


def from_owners(value, owners, extra):
    devices = lax.axis_size("seq")
    count = value.shape[0]
    chunks = value.reshape(count, devices, -1).transpose(1, 0, 2).reshape(devices, -1)
    width = chunks.shape[1]
    packed = jnp.concatenate([chunks, extra.astype(value.dtype)], axis=1)
    got = lax.all_to_all(packed, "seq", 0, 0, tiled=True)
    rows = got[:, :width].reshape(devices, count, -1)
    mine = jnp.stack([rows[owners[i], i] for i in range(count)])
    full = lax.all_gather(mine, "seq", axis=0, tiled=False)
    return full.transpose(1, 0, 2).reshape(value.shape), got[:, width:].astype(extra.dtype)


def summed_to_all(value):
    devices = lax.axis_size("seq")
    chunks = value.astype(jnp.bfloat16).reshape(devices, -1)
    got = lax.all_to_all(chunks, "seq", 0, 0, tiled=True)
    total = jnp.sum(got.astype(jnp.float32), axis=0).astype(jnp.bfloat16)
    full = lax.all_gather(total, "seq", axis=0, tiled=True)
    return full.reshape(value.shape).astype(jnp.float32)


def head_blocks(matrix, blocks):
    return matrix.reshape(blocks, BLK, H, HD).transpose(0, 2, 1, 3)


def token_rows(blocked):
    blocks = blocked.shape[0]
    return blocked.transpose(0, 2, 1, 3).reshape(blocks * BLK, H * HD)


def pair_heads(rows, blocks):
    return (
        rows.reshape(blocks, BLK, 2, H, HD).transpose(0, 3, 1, 2, 4).reshape(blocks, H, BLK, 2 * HD)
    )


def slot_plan(block_lists, per_dev, devices, head_ids):
    owners = (block_lists // per_dev).reshape(-1)
    req_codes = (block_lists % per_dev * H + head_ids[None, :, None]).reshape(-1)
    onehot = (owners[:, None] == jnp.arange(devices, dtype=jnp.int32)[None, :]).astype(jnp.int32)
    before = jnp.cumsum(onehot, axis=0) - onehot
    return (owners, jnp.sum(before * onehot, axis=1), req_codes)


def sparse_group(query_g, grad_g, keyvals, allowed, factor):
    key_part = keyvals[..., :HD]
    value_part = keyvals[..., HD:]
    scores = (
        jnp.einsum("ghqd,ghkd->ghqk", query_g, key_part, preferred_element_type=jnp.float32)
        * factor
    )
    mask = allowed[:, :, None, :]
    row_max = jnp.max(jnp.where(mask, scores, -1e30), axis=-1, keepdims=True)
    expo = jnp.where(mask, jnp.exp(scores - row_max), 0.0)
    totals = jnp.sum(expo, axis=-1, keepdims=True)
    result = (
        jnp.einsum(
            "ghqk,ghkd->ghqd",
            expo.astype(jnp.bfloat16),
            value_part,
            preferred_element_type=jnp.float32,
        )
        / totals
    )
    probs = expo / totals
    dprobs = jnp.einsum("ghqd,ghkd->ghqk", grad_g, value_part, preferred_element_type=jnp.float32)
    dotted = jnp.sum(grad_g.astype(jnp.float32) * result, axis=-1, keepdims=True)
    dscore = (probs * (dprobs - dotted)).astype(jnp.bfloat16)
    dquery = factor * jnp.einsum(
        "ghqk,ghkd->ghqd", dscore, key_part, preferred_element_type=jnp.float32
    )
    dkey = factor * jnp.einsum(
        "ghqk,ghqd->ghkd", dscore, query_g, preferred_element_type=jnp.float32
    )
    dvalue = jnp.einsum(
        "ghqk,ghqd->ghkd", probs.astype(jnp.bfloat16), grad_g, preferred_element_type=jnp.float32
    )
    stats = jnp.stack([row_max[..., 0], totals[..., 0], dotted[..., 0]], axis=1)
    return (result, dquery, jnp.concatenate([dkey, dvalue], axis=-1), stats)


def sparse_kernel(q_ref, g_ref, kv_ref, allow_ref, out_ref, dq_ref, terms_ref, *, factor):
    nt = (((1,), (1,)), ((), ()))
    for head in range(q_ref.shape[1]):
        query = q_ref[0, head]
        grad = g_ref[0, head]
        keyval = kv_ref[0, head]
        key = keyval[:, :HD]
        value = keyval[:, HD:]
        scores = lax.dot_general(query, key, nt, preferred_element_type=jnp.float32) * factor
        mask = allow_ref[0, head] > 0.5
        row_max = jnp.max(jnp.where(mask, scores, -1e30), axis=-1, keepdims=True)
        expo = jnp.where(mask, jnp.exp(scores - row_max), 0.0)
        totals = jnp.sum(expo, axis=-1, keepdims=True)
        result = (
            jnp.dot(expo.astype(jnp.bfloat16), value, preferred_element_type=jnp.float32)
            / totals
        )
        probs = expo / totals
        dprobs = lax.dot_general(grad, value, nt, preferred_element_type=jnp.float32)
        dotted = jnp.sum(grad.astype(jnp.float32) * result, axis=-1, keepdims=True)
        dscore = probs * (dprobs - dotted)
        dq = factor * jnp.dot(dscore.astype(jnp.bfloat16), key, preferred_element_type=jnp.float32)
        dkey = factor * jnp.dot(
            dscore.astype(jnp.bfloat16).T, query, preferred_element_type=jnp.float32
        )
        dvalue = jnp.dot(probs.astype(jnp.bfloat16).T, grad, preferred_element_type=jnp.float32)
        out_ref[0, head] = result
        dq_ref[0, head] = dq
        terms_ref[0, head, :, :HD] = dkey
        terms_ref[0, head, :, HD:] = dvalue


def sparse_call(query_h, grad_h, keyvals, allowed_f, factor, interpret=False, per_step=6):
    blocks, heads, rows, _ = query_h.shape
    keys_n = keyvals.shape[2]
    small = pl.BlockSpec((1, per_step, rows, HD), lambda i, h: (i, h, 0, 0))
    return pl.pallas_call(
        lambda *refs: sparse_kernel(*refs, factor=factor),
        grid=(blocks, heads // per_step),
        in_specs=[
            small,
            small,
            pl.BlockSpec((1, per_step, keys_n, 2 * HD), lambda i, h: (i, h, 0, 0)),
            pl.BlockSpec((1, per_step, 1, keys_n), lambda i, h: (i, h, 0, 0)),
        ],
        out_specs=[
            small,
            small,
            pl.BlockSpec((1, per_step, keys_n, 2 * HD), lambda i, h: (i, h, 0, 0)),
        ],
        out_shape=[
            jax.ShapeDtypeStruct((blocks, heads, rows, HD), jnp.float32),
            jax.ShapeDtypeStruct((blocks, heads, rows, HD), jnp.float32),
            jax.ShapeDtypeStruct((blocks, heads, keys_n, 2 * HD), jnp.float32),
        ],
        interpret=interpret,
    )(query_h, grad_h, keyvals, allowed_f)


def per_device(queries, keys, values, out_grad, random_blocks, global_blocks):
    tokens = queries.shape[0]
    width = queries.shape[1]
    per_dev = tokens // BLK
    devices = lax.axis_size("seq")
    me_index = lax.axis_index("seq")
    blocks_all = per_dev * devices
    factor = 1.0 / math.sqrt(HD)
    entry_count = per_dev * H * R
    capacity = (entry_count + devices - 2) // (devices - 1) + 4
    head_ids = jnp.arange(H, dtype=jnp.int32)
    block_ids = me_index * per_dev + jnp.arange(per_dev, dtype=jnp.int32)
    is_global = jnp.any(block_ids[:, None] == global_blocks[None, :], axis=1)
    row_global = jnp.repeat(is_global, BLK)
    masked = jnp.where(row_global[:, None], jnp.zeros_like(out_grad), out_grad)
    kv_rows = jnp.concatenate([keys, values], axis=1)
    edge_rows = jnp.concatenate([kv_rows[:BLK], kv_rows[-BLK:]], axis=0)
    padded = padded_2(edge_rows, (("seq", 0),), BLK)
    left_rows = padded[:BLK]
    right_rows = padded[3 * BLK :]
    extended = jnp.concatenate(
        [
            left_rows[None, :, : 2 * width],
            kv_rows.reshape(per_dev, BLK, 2 * width),
            right_rows[None, :, : 2 * width],
        ],
        axis=0,
    )
    kv_heads = pair_heads(extended, per_dev + 2)
    kv_local = kv_heads[1 : per_dev + 1]
    global_rows = []
    for number in range(NG):
        row_start = global_blocks[number] % per_dev * BLK
        global_rows.append(
            jnp.concatenate(
                [
                    lax.dynamic_slice_in_dim(source, row_start, BLK, 0)
                    for source in (queries, keys, values, out_grad)
                ],
                axis=1,
            )
        )
    stacked_rows = jnp.stack(global_rows)
    owners, slot_ids, req_codes = slot_plan(random_blocks, per_dev, devices, head_ids)
    slot_key = owners * capacity + slot_ids
    slot_hit = jnp.arange(devices * capacity, dtype=jnp.int32)[:, None] == slot_key[None, :]
    outgoing = jnp.where(
        jnp.any(slot_hit, axis=1), jnp.sum(jnp.where(slot_hit, req_codes[None, :], 0), axis=1), -1
    ).reshape(devices, capacity)
    grows, wanted = from_owners(stacked_rows, global_blocks // per_dev, outgoing)
    sending = kv_local.reshape(per_dev * H, BLK, 2 * HD)[jnp.maximum(wanted, 0)]
    g_query = grows[:, :, :width].reshape(NG, BLK, H, HD)
    g_grad = grows[:, :, 3 * width :].reshape(NG, BLK, H, HD)
    g_kv = pair_heads(grows[:, :, width : 3 * width], NG)
    fetched = lax.all_to_all(sending, "seq", split_axis=0, concat_axis=0, tiled=True)
    rand_kv = fetched[owners, slot_ids].reshape(per_dev, H, R, BLK, 2 * HD)
    shifts = jnp.arange(-1, 2, dtype=jnp.int32)
    window_ids = (block_ids[:, None] + shifts[None, :]) % blocks_all
    other_ids = jnp.concatenate(
        [jnp.broadcast_to(window_ids[:, None, :], (per_dev, H, 3)), random_blocks], axis=2
    )
    global_kept = jnp.all(global_blocks[None, None, :, None] != other_ids[:, :, None, :], axis=3)
    allowed = jnp.concatenate(
        [jnp.ones((per_dev, H, 3), jnp.bool_), global_kept, jnp.ones((per_dev, H, R), jnp.bool_)],
        axis=2,
    )
    allowed = jnp.repeat(allowed, BLK, axis=2)
    query_heads = head_blocks(queries, per_dev)
    grad_heads = head_blocks(masked, per_dev)
    group = QGROUP
    groups = per_dev // group
    glob_slots = jnp.broadcast_to(g_kv.transpose(1, 0, 2, 3)[None], (group, H, NG, BLK, 2 * HD))

    def run_group(number):
        win_slots = jnp.stack(
            [kv_heads[0:group], kv_heads[1 : group + 1], kv_heads[2 : group + 2]], axis=2
        )
        keyvals = jnp.concatenate([win_slots, glob_slots, rand_kv], axis=2).reshape(
            group, H, SLOTS * BLK, 2 * HD
        )
        result, dquery, terms = sparse_call(
            query_heads, grad_heads, keyvals, allowed.astype(jnp.float32)[:, :, None, :], factor
        )
        terms = terms.reshape(group, H, SLOTS, BLK, 2 * HD)
        spacing = ((0, 0), (0, 0), (0, 0), (0, 0))
        window_sum = (
            jnp.pad(terms[:, :, 0], ((0, 2),) + spacing[1:])
            + jnp.pad(terms[:, :, 1], ((1, 1),) + spacing[1:])
            + jnp.pad(terms[:, :, 2], ((2, 0),) + spacing[1:])
        )
        global_sum = jnp.sum(terms[:, :, 3 : 3 + NG], axis=0)
        random_out = terms[:, :, 3 + NG :].astype(jnp.bfloat16)
        return (result, dquery, window_sum, global_sum, random_out)

    if groups == 1:
        mapped = tuple(part[None] for part in run_group(0))
    else:
        mapped = lax.map(run_group, jnp.arange(groups, dtype=jnp.int32))
    result = mapped[0].reshape(per_dev, H, BLK, HD)
    dquery = mapped[1].reshape(per_dev, H, BLK, HD)
    place = (
        jnp.arange(groups, dtype=jnp.int32)[:, None] * group
        + jnp.arange(group + 2, dtype=jnp.int32)[None, :]
    ).reshape(-1)
    if groups == 1:
        padded_grads = mapped[2].reshape(per_dev + 2, H, BLK, 2 * HD)
    else:
        padded_grads = (
            jnp.zeros((per_dev + 2, H, BLK, 2 * HD), jnp.float32)
            .at[place]
            .add(mapped[2].reshape(-1, H, BLK, 2 * HD))
        )
    global_part = jnp.sum(mapped[3], axis=0).transpose(1, 0, 2, 3)
    random_out = mapped[4].reshape(-1, BLK, 2 * HD)
    own_grads = padded_grads[1 : per_dev + 1]
    edge_pair = jnp.stack([padded_grads[0], padded_grads[per_dev + 1]])
    near_grads = padded_2(edge_pair.astype(jnp.bfloat16), (("seq", 0),), 1).astype(edge_pair.dtype)
    own_grads = own_grads.at[0].add(near_grads[0]).at[per_dev - 1].add(near_grads[3])
    back_buffer = jnp.einsum(
        "se,ef->sf",
        slot_hit.astype(jnp.bfloat16),
        random_out.reshape(-1, BLK * 2 * HD),
        preferred_element_type=jnp.bfloat16,
    ).reshape(devices, capacity, BLK, 2 * HD)
    returned = lax.all_to_all(back_buffer, "seq", split_axis=0, concat_axis=0, tiled=True)
    code_hit = (
        wanted.reshape(-1)[:, None] == jnp.arange(per_dev * H, dtype=jnp.int32)[None, :]
    ).astype(jnp.bfloat16)
    table_grads = jnp.einsum(
        "sc,sf->cf",
        code_hit,
        returned.reshape(-1, BLK * 2 * HD),
        preferred_element_type=jnp.float32,
    ).reshape(per_dev * H, BLK, 2 * HD)
    own_grads = own_grads + table_grads.reshape(per_dev, H, BLK, 2 * HD)
    key_tok = keys.reshape(tokens, H, HD)
    value_tok = values.reshape(tokens, H, HD)
    scores = (
        jnp.einsum("gqhd,khd->ghqk", g_query, key_tok, preferred_element_type=jnp.float32) * factor
    )
    local_max = jnp.max(scores, axis=-1)
    local_expo = jnp.exp(scores - local_max[..., None])
    part_acc = jnp.einsum(
        "ghqk,khd->ghqd",
        local_expo.astype(jnp.bfloat16),
        value_tok,
        preferred_element_type=jnp.float32,
    )
    row_shape = local_max.shape
    packed = jnp.concatenate(
        [local_max[..., None], jnp.sum(local_expo, axis=-1)[..., None], part_acc], axis=-1
    ).reshape(devices, -1, HD + 2)
    got = lax.all_to_all(packed, "seq", 0, 0, tiled=True)
    top = jnp.max(got[..., 0], axis=0)
    scale = jnp.exp(got[..., 0] - top[None])
    tot = jnp.sum(scale * got[..., 1], axis=0)
    acc = jnp.sum(scale[..., None] * got[..., 2:], axis=0) / tot[:, None]
    merged = lax.all_gather(
        jnp.concatenate([top[:, None], tot[:, None], acc], axis=-1), "seq", axis=0, tiled=True
    )
    row_top = merged[:, 0].reshape(row_shape)
    row_tot = merged[:, 1].reshape(row_shape)
    global_out = merged[:, 2:].reshape(row_shape + (HD,))
    probs = jnp.exp(scores - row_top[..., None]) / row_tot[..., None]
    dprobs = jnp.einsum("gqhd,khd->ghqk", g_grad, value_tok, preferred_element_type=jnp.float32)
    dotted = jnp.sum(g_grad.transpose(0, 2, 1, 3).astype(jnp.float32) * global_out, axis=-1)
    dscore = (probs * (dprobs - dotted[..., None])).astype(jnp.bfloat16)
    g_dquery = factor * jnp.einsum(
        "ghqk,khd->ghqd", dscore, key_tok, preferred_element_type=jnp.float32
    )
    tok_dkey = factor * jnp.einsum(
        "ghqk,gqhd->khd", dscore, g_query, preferred_element_type=jnp.float32
    )
    tok_dvalue = jnp.einsum(
        "ghqk,gqhd->khd", probs.astype(jnp.bfloat16), g_grad, preferred_element_type=jnp.float32
    )
    both_sum = summed_to_all(jnp.concatenate([g_dquery, global_part], axis=-1))
    dquery_sum = both_sum[..., :HD]
    global_sum = both_sum[..., HD:]
    for number in range(NG):
        owned = global_blocks[number] // per_dev == me_index
        local_block = global_blocks[number] % per_dev
        result = result.at[local_block].set(
            jnp.where(owned, global_out[number], result[local_block])
        )
        dquery = dquery.at[local_block].add(jnp.where(owned, dquery_sum[number], 0.0))
        own_grads = own_grads.at[local_block].add(jnp.where(owned, global_sum[number], 0.0))
    attended = token_rows(result).astype(jnp.bfloat16)
    query_grad = token_rows(dquery).astype(jnp.bfloat16)
    key_grad = (token_rows(own_grads[..., :HD]) + tok_dkey.reshape(tokens, width)).astype(
        jnp.bfloat16
    )
    value_grad = (token_rows(own_grads[..., HD:]) + tok_dvalue.reshape(tokens, width)).astype(
        jnp.bfloat16
    )
    return (attended, query_grad, key_grad, value_grad)


def solution(mesh):
    return jax.shard_map(
        per_device,
        mesh=mesh,
        in_specs=(
            P(("grp", "seq"), None),
            P(("grp", "seq"), None),
            P(("grp", "seq"), None),
            P(("grp", "seq"), None),
            P(("grp", "seq"), None, None),
            P("grp"),
        ),
        out_specs=(
            P(("grp", "seq"), None),
            P(("grp", "seq"), None),
            P(("grp", "seq"), None),
            P(("grp", "seq"), None),
        ),
        check_vma=False,
    )
```

```python
import math

import jax
import jax.numpy as jnp
from jax import lax
from jax.experimental import pallas as pl
from jax.sharding import PartitionSpec as P

H = 12
HD = 64
BLK = 64
R = 3
NG = 2
QGROUP = 8
SLOTS = 8


def padded_2(block, sides, width):
    for axis, dim in sides:
        count = lax.axis_size(axis)
        forward = [(i, i + 1) for i in range(count - 1)]
        forward.append((count - 1, 0))
        backward = [(target, source) for source, target in forward]
        low = lax.ppermute(
            lax.slice_in_dim(block, block.shape[dim] - width, None, axis=dim), axis, forward
        )
        high = lax.ppermute(lax.slice_in_dim(block, 0, width, axis=dim), axis, backward)
        block = jnp.concatenate([low, block, high], axis=dim)
    return block


def from_owners(value, owners, extra):
    devices = lax.axis_size("seq")
    count = value.shape[0]
    chunks = value.reshape(count, devices, -1).transpose(1, 0, 2).reshape(devices, -1)
    width = chunks.shape[1]
    packed = jnp.concatenate([chunks, extra.astype(value.dtype)], axis=1)
    got = lax.all_to_all(packed, "seq", 0, 0, tiled=True)
    rows = got[:, :width].reshape(devices, count, -1)
    mine = jnp.stack([rows[owners[i], i] for i in range(count)])
    full = lax.all_gather(mine, "seq", axis=0, tiled=False)
    return full.transpose(1, 0, 2).reshape(value.shape), got[:, width:].astype(extra.dtype)


def summed_to_all(value):
    devices = lax.axis_size("seq")
    chunks = value.astype(jnp.bfloat16).reshape(devices, -1)
    got = lax.all_to_all(chunks, "seq", 0, 0, tiled=True)
    total = jnp.sum(got.astype(jnp.float32), axis=0).astype(jnp.bfloat16)
    full = lax.all_gather(total, "seq", axis=0, tiled=True)
    return full.reshape(value.shape).astype(jnp.float32)


def head_blocks(matrix, blocks):
    return matrix.reshape(blocks, BLK, H, HD).transpose(0, 2, 1, 3)


def token_rows(blocked):
    blocks = blocked.shape[0]
    return blocked.transpose(0, 2, 1, 3).reshape(blocks * BLK, H * HD)


def pair_heads(rows, blocks):
    return (
        rows.reshape(blocks, BLK, 2, H, HD).transpose(0, 3, 1, 2, 4).reshape(blocks, H, BLK, 2 * HD)
    )


def slot_plan(block_lists, per_dev, devices, head_ids):
    owners = (block_lists // per_dev).reshape(-1)
    req_codes = (block_lists % per_dev * H + head_ids[None, :, None]).reshape(-1)
    onehot = (owners[:, None] == jnp.arange(devices, dtype=jnp.int32)[None, :]).astype(jnp.int32)
    before = jnp.cumsum(onehot, axis=0) - onehot
    return (owners, jnp.sum(before * onehot, axis=1), req_codes)


def sparse_group(query_g, grad_g, keyvals, allowed, factor):
    key_part = keyvals[..., :HD]
    value_part = keyvals[..., HD:]
    scores = (
        jnp.einsum("ghqd,ghkd->ghqk", query_g, key_part, preferred_element_type=jnp.float32)
        * factor
    )
    mask = allowed[:, :, None, :]
    row_max = jnp.max(jnp.where(mask, scores, -1e30), axis=-1, keepdims=True)
    expo = jnp.where(mask, jnp.exp(scores - row_max), 0.0)
    totals = jnp.sum(expo, axis=-1, keepdims=True)
    result = (
        jnp.einsum(
            "ghqk,ghkd->ghqd",
            expo.astype(jnp.bfloat16),
            value_part,
            preferred_element_type=jnp.float32,
        )
        / totals
    )
    probs = expo / totals
    dprobs = jnp.einsum("ghqd,ghkd->ghqk", grad_g, value_part, preferred_element_type=jnp.float32)
    dotted = jnp.sum(grad_g.astype(jnp.float32) * result, axis=-1, keepdims=True)
    dscore = (probs * (dprobs - dotted)).astype(jnp.bfloat16)
    dquery = factor * jnp.einsum(
        "ghqk,ghkd->ghqd", dscore, key_part, preferred_element_type=jnp.float32
    )
    dkey = factor * jnp.einsum(
        "ghqk,ghqd->ghkd", dscore, query_g, preferred_element_type=jnp.float32
    )
    dvalue = jnp.einsum(
        "ghqk,ghqd->ghkd", probs.astype(jnp.bfloat16), grad_g, preferred_element_type=jnp.float32
    )
    stats = jnp.stack([row_max[..., 0], totals[..., 0], dotted[..., 0]], axis=1)
    return (result, dquery, jnp.concatenate([dkey, dvalue], axis=-1), stats)


def sparse_kernel(q_ref, g_ref, kv_ref, allow_ref, out_ref, dq_ref, win_ref, glob_ref, rand_ref, *, factor):
    nt = (((1,), (1,)), ((), ()))
    for head in range(q_ref.shape[1]):
        query = q_ref[0, head]
        grad = g_ref[0, head]
        keyval = kv_ref[0, head]
        key = keyval[:, :HD]
        value = keyval[:, HD:]
        scores = lax.dot_general(query, key, nt, preferred_element_type=jnp.float32) * factor
        mask = allow_ref[0, head] > 0.5
        row_max = jnp.max(jnp.where(mask, scores, -1e30), axis=-1, keepdims=True)
        expo = jnp.where(mask, jnp.exp(scores - row_max), 0.0)
        totals = jnp.sum(expo, axis=-1, keepdims=True)
        result = (
            jnp.dot(expo.astype(jnp.bfloat16), value, preferred_element_type=jnp.float32)
            / totals
        )
        probs = expo / totals
        dprobs = lax.dot_general(grad, value, nt, preferred_element_type=jnp.float32)
        dotted = jnp.sum(grad.astype(jnp.float32) * result, axis=-1, keepdims=True)
        dscore = probs * (dprobs - dotted)
        dq = factor * jnp.dot(dscore.astype(jnp.bfloat16), key, preferred_element_type=jnp.float32)
        dkey = factor * jnp.dot(
            dscore.astype(jnp.bfloat16).T, query, preferred_element_type=jnp.float32
        )
        dvalue = jnp.dot(probs.astype(jnp.bfloat16).T, grad, preferred_element_type=jnp.float32)
        out_ref[0, head] = result
        dq_ref[0, head] = dq
        kinds = ((win_ref, 0, jnp.float32), (glob_ref, 3, jnp.float32), (rand_ref, 5, jnp.bfloat16))
        for target, first, kind in kinds:
            for slot in range(target.shape[2]):
                rows = slice((first + slot) * BLK, (first + slot + 1) * BLK)
                target[0, head, slot, :, :HD] = dkey[rows].astype(kind)
                target[0, head, slot, :, HD:] = dvalue[rows].astype(kind)


def sparse_call(query_h, grad_h, keyvals, allowed_f, factor, interpret=False, per_step=6):
    blocks, heads, rows, _ = query_h.shape
    keys_n = keyvals.shape[2]
    small = pl.BlockSpec((1, per_step, rows, HD), lambda i, h: (i, h, 0, 0))
    return pl.pallas_call(
        lambda *refs: sparse_kernel(*refs, factor=factor),
        grid=(blocks, heads // per_step),
        in_specs=[
            small,
            small,
            pl.BlockSpec((1, per_step, keys_n, 2 * HD), lambda i, h: (i, h, 0, 0)),
            pl.BlockSpec((1, per_step, 1, keys_n), lambda i, h: (i, h, 0, 0)),
        ],
        out_specs=[
            small,
            small,
            pl.BlockSpec((1, per_step, 3, BLK, 2 * HD), lambda i, h: (i, h, 0, 0, 0)),
            pl.BlockSpec((1, per_step, NG, BLK, 2 * HD), lambda i, h: (i, h, 0, 0, 0)),
            pl.BlockSpec((1, per_step, R, BLK, 2 * HD), lambda i, h: (i, h, 0, 0, 0)),
        ],
        out_shape=[
            jax.ShapeDtypeStruct((blocks, heads, rows, HD), jnp.float32),
            jax.ShapeDtypeStruct((blocks, heads, rows, HD), jnp.float32),
            jax.ShapeDtypeStruct((blocks, heads, 3, BLK, 2 * HD), jnp.float32),
            jax.ShapeDtypeStruct((blocks, heads, NG, BLK, 2 * HD), jnp.float32),
            jax.ShapeDtypeStruct((blocks, heads, R, BLK, 2 * HD), jnp.bfloat16),
        ],
        interpret=interpret,
    )(query_h, grad_h, keyvals, allowed_f)


def per_device(queries, keys, values, out_grad, random_blocks, global_blocks):
    tokens = queries.shape[0]
    width = queries.shape[1]
    per_dev = tokens // BLK
    devices = lax.axis_size("seq")
    me_index = lax.axis_index("seq")
    blocks_all = per_dev * devices
    factor = 1.0 / math.sqrt(HD)
    entry_count = per_dev * H * R
    capacity = (entry_count + devices - 2) // (devices - 1) + 4
    head_ids = jnp.arange(H, dtype=jnp.int32)
    block_ids = me_index * per_dev + jnp.arange(per_dev, dtype=jnp.int32)
    is_global = jnp.any(block_ids[:, None] == global_blocks[None, :], axis=1)
    row_global = jnp.repeat(is_global, BLK)
    masked = jnp.where(row_global[:, None], jnp.zeros_like(out_grad), out_grad)
    kv_rows = jnp.concatenate([keys, values], axis=1)
    edge_rows = jnp.concatenate([kv_rows[:BLK], kv_rows[-BLK:]], axis=0)
    padded = padded_2(edge_rows, (("seq", 0),), BLK)
    left_rows = padded[:BLK]
    right_rows = padded[3 * BLK :]
    extended = jnp.concatenate(
        [
            left_rows[None, :, : 2 * width],
            kv_rows.reshape(per_dev, BLK, 2 * width),
            right_rows[None, :, : 2 * width],
        ],
        axis=0,
    )
    kv_heads = pair_heads(extended, per_dev + 2)
    kv_local = kv_heads[1 : per_dev + 1]
    global_rows = []
    for number in range(NG):
        row_start = global_blocks[number] % per_dev * BLK
        global_rows.append(
            jnp.concatenate(
                [
                    lax.dynamic_slice_in_dim(source, row_start, BLK, 0)
                    for source in (queries, keys, values, out_grad)
                ],
                axis=1,
            )
        )
    stacked_rows = jnp.stack(global_rows)
    owners, slot_ids, req_codes = slot_plan(random_blocks, per_dev, devices, head_ids)
    slot_key = owners * capacity + slot_ids
    slot_hit = jnp.arange(devices * capacity, dtype=jnp.int32)[:, None] == slot_key[None, :]
    outgoing = jnp.where(
        jnp.any(slot_hit, axis=1), jnp.sum(jnp.where(slot_hit, req_codes[None, :], 0), axis=1), -1
    ).reshape(devices, capacity)
    grows, wanted = from_owners(stacked_rows, global_blocks // per_dev, outgoing)
    sending = kv_local.reshape(per_dev * H, BLK, 2 * HD)[jnp.maximum(wanted, 0)]
    g_query = grows[:, :, :width].reshape(NG, BLK, H, HD)
    g_grad = grows[:, :, 3 * width :].reshape(NG, BLK, H, HD)
    g_kv = pair_heads(grows[:, :, width : 3 * width], NG)
    fetched = lax.all_to_all(sending, "seq", split_axis=0, concat_axis=0, tiled=True)
    rand_kv = fetched[owners, slot_ids].reshape(per_dev, H, R, BLK, 2 * HD)
    shifts = jnp.arange(-1, 2, dtype=jnp.int32)
    window_ids = (block_ids[:, None] + shifts[None, :]) % blocks_all
    other_ids = jnp.concatenate(
        [jnp.broadcast_to(window_ids[:, None, :], (per_dev, H, 3)), random_blocks], axis=2
    )
    global_kept = jnp.all(global_blocks[None, None, :, None] != other_ids[:, :, None, :], axis=3)
    allowed = jnp.concatenate(
        [jnp.ones((per_dev, H, 3), jnp.bool_), global_kept, jnp.ones((per_dev, H, R), jnp.bool_)],
        axis=2,
    )
    allowed = jnp.repeat(allowed, BLK, axis=2)
    query_heads = head_blocks(queries, per_dev)
    grad_heads = head_blocks(masked, per_dev)
    group = QGROUP
    groups = per_dev // group
    glob_slots = jnp.broadcast_to(g_kv.transpose(1, 0, 2, 3)[None], (group, H, NG, BLK, 2 * HD))

    def run_group(number):
        win_slots = jnp.stack(
            [kv_heads[0:group], kv_heads[1 : group + 1], kv_heads[2 : group + 2]], axis=2
        )
        keyvals = jnp.concatenate([win_slots, glob_slots, rand_kv], axis=2).reshape(
            group, H, SLOTS * BLK, 2 * HD
        )
        result, dquery, win_terms, glob_terms, random_out = sparse_call(
            query_heads, grad_heads, keyvals, allowed.astype(jnp.float32)[:, :, None, :], factor
        )
        spacing = ((0, 0), (0, 0), (0, 0), (0, 0))
        window_sum = (
            jnp.pad(win_terms[:, :, 0], ((0, 2),) + spacing[1:])
            + jnp.pad(win_terms[:, :, 1], ((1, 1),) + spacing[1:])
            + jnp.pad(win_terms[:, :, 2], ((2, 0),) + spacing[1:])
        )
        global_sum = jnp.sum(glob_terms, axis=0)
        return (result, dquery, window_sum, global_sum, random_out)

    if groups == 1:
        mapped = tuple(part[None] for part in run_group(0))
    else:
        mapped = lax.map(run_group, jnp.arange(groups, dtype=jnp.int32))
    result = mapped[0].reshape(per_dev, H, BLK, HD)
    dquery = mapped[1].reshape(per_dev, H, BLK, HD)
    place = (
        jnp.arange(groups, dtype=jnp.int32)[:, None] * group
        + jnp.arange(group + 2, dtype=jnp.int32)[None, :]
    ).reshape(-1)
    if groups == 1:
        padded_grads = mapped[2].reshape(per_dev + 2, H, BLK, 2 * HD)
    else:
        padded_grads = (
            jnp.zeros((per_dev + 2, H, BLK, 2 * HD), jnp.float32)
            .at[place]
            .add(mapped[2].reshape(-1, H, BLK, 2 * HD))
        )
    global_part = jnp.sum(mapped[3], axis=0).transpose(1, 0, 2, 3)
    random_out = mapped[4].reshape(-1, BLK, 2 * HD)
    own_grads = padded_grads[1 : per_dev + 1]
    edge_pair = jnp.stack([padded_grads[0], padded_grads[per_dev + 1]])
    near_grads = padded_2(edge_pair.astype(jnp.bfloat16), (("seq", 0),), 1).astype(edge_pair.dtype)
    own_grads = own_grads.at[0].add(near_grads[0]).at[per_dev - 1].add(near_grads[3])
    back_buffer = jnp.einsum(
        "se,ef->sf",
        slot_hit.astype(jnp.bfloat16),
        random_out.reshape(-1, BLK * 2 * HD),
        preferred_element_type=jnp.bfloat16,
    ).reshape(devices, capacity, BLK, 2 * HD)
    returned = lax.all_to_all(back_buffer, "seq", split_axis=0, concat_axis=0, tiled=True)
    code_hit = (
        wanted.reshape(-1)[:, None] == jnp.arange(per_dev * H, dtype=jnp.int32)[None, :]
    ).astype(jnp.bfloat16)
    table_grads = jnp.einsum(
        "sc,sf->cf",
        code_hit,
        returned.reshape(-1, BLK * 2 * HD),
        preferred_element_type=jnp.float32,
    ).reshape(per_dev * H, BLK, 2 * HD)
    own_grads = own_grads + table_grads.reshape(per_dev, H, BLK, 2 * HD)
    key_tok = keys.reshape(tokens, H, HD)
    value_tok = values.reshape(tokens, H, HD)
    scores = (
        jnp.einsum("gqhd,khd->ghqk", g_query, key_tok, preferred_element_type=jnp.float32) * factor
    )
    local_max = jnp.max(scores, axis=-1)
    local_expo = jnp.exp(scores - local_max[..., None])
    part_acc = jnp.einsum(
        "ghqk,khd->ghqd",
        local_expo.astype(jnp.bfloat16),
        value_tok,
        preferred_element_type=jnp.float32,
    )
    row_shape = local_max.shape
    packed = jnp.concatenate(
        [local_max[..., None], jnp.sum(local_expo, axis=-1)[..., None], part_acc], axis=-1
    ).reshape(devices, -1, HD + 2)
    got = lax.all_to_all(packed, "seq", 0, 0, tiled=True)
    top = jnp.max(got[..., 0], axis=0)
    scale = jnp.exp(got[..., 0] - top[None])
    tot = jnp.sum(scale * got[..., 1], axis=0)
    acc = jnp.sum(scale[..., None] * got[..., 2:], axis=0) / tot[:, None]
    merged = lax.all_gather(
        jnp.concatenate([top[:, None], tot[:, None], acc], axis=-1), "seq", axis=0, tiled=True
    )
    row_top = merged[:, 0].reshape(row_shape)
    row_tot = merged[:, 1].reshape(row_shape)
    global_out = merged[:, 2:].reshape(row_shape + (HD,))
    probs = jnp.exp(scores - row_top[..., None]) / row_tot[..., None]
    dprobs = jnp.einsum("gqhd,khd->ghqk", g_grad, value_tok, preferred_element_type=jnp.float32)
    dotted = jnp.sum(g_grad.transpose(0, 2, 1, 3).astype(jnp.float32) * global_out, axis=-1)
    dscore = (probs * (dprobs - dotted[..., None])).astype(jnp.bfloat16)
    g_dquery = factor * jnp.einsum(
        "ghqk,khd->ghqd", dscore, key_tok, preferred_element_type=jnp.float32
    )
    tok_dkey = factor * jnp.einsum(
        "ghqk,gqhd->khd", dscore, g_query, preferred_element_type=jnp.float32
    )
    tok_dvalue = jnp.einsum(
        "ghqk,gqhd->khd", probs.astype(jnp.bfloat16), g_grad, preferred_element_type=jnp.float32
    )
    both_sum = summed_to_all(jnp.concatenate([g_dquery, global_part], axis=-1))
    dquery_sum = both_sum[..., :HD]
    global_sum = both_sum[..., HD:]
    for number in range(NG):
        owned = global_blocks[number] // per_dev == me_index
        local_block = global_blocks[number] % per_dev
        result = result.at[local_block].set(
            jnp.where(owned, global_out[number], result[local_block])
        )
        dquery = dquery.at[local_block].add(jnp.where(owned, dquery_sum[number], 0.0))
        own_grads = own_grads.at[local_block].add(jnp.where(owned, global_sum[number], 0.0))
    attended = token_rows(result).astype(jnp.bfloat16)
    query_grad = token_rows(dquery).astype(jnp.bfloat16)
    key_grad = (token_rows(own_grads[..., :HD]) + tok_dkey.reshape(tokens, width)).astype(
        jnp.bfloat16
    )
    value_grad = (token_rows(own_grads[..., HD:]) + tok_dvalue.reshape(tokens, width)).astype(
        jnp.bfloat16
    )
    return (attended, query_grad, key_grad, value_grad)


def solution(mesh):
    return jax.shard_map(
        per_device,
        mesh=mesh,
        in_specs=(
            P(("grp", "seq"), None),
            P(("grp", "seq"), None),
            P(("grp", "seq"), None),
            P(("grp", "seq"), None),
            P(("grp", "seq"), None, None),
            P("grp"),
        ),
        out_specs=(
            P(("grp", "seq"), None),
            P(("grp", "seq"), None),
            P(("grp", "seq"), None),
            P(("grp", "seq"), None),
        ),
        check_vma=False,
    )
```

```python
import math

import jax
import jax.numpy as jnp
from jax import lax
from jax.experimental import pallas as pl
from jax.sharding import PartitionSpec as P

H = 12
HD = 64
BLK = 64
R = 3
NG = 2
QGROUP = 8
SLOTS = 8


def padded_2(block, sides, width):
    for axis, dim in sides:
        count = lax.axis_size(axis)
        forward = [(i, i + 1) for i in range(count - 1)]
        forward.append((count - 1, 0))
        backward = [(target, source) for source, target in forward]
        low = lax.ppermute(
            lax.slice_in_dim(block, block.shape[dim] - width, None, axis=dim), axis, forward
        )
        high = lax.ppermute(lax.slice_in_dim(block, 0, width, axis=dim), axis, backward)
        block = jnp.concatenate([low, block, high], axis=dim)
    return block


def from_owners(value, owners, extra):
    devices = lax.axis_size("seq")
    count = value.shape[0]
    chunks = value.reshape(count, devices, -1).transpose(1, 0, 2).reshape(devices, -1)
    width = chunks.shape[1]
    packed = jnp.concatenate([chunks, extra.astype(value.dtype)], axis=1)
    got = lax.all_to_all(packed, "seq", 0, 0, tiled=True)
    rows = got[:, :width].reshape(devices, count, -1)
    mine = jnp.stack([rows[owners[i], i] for i in range(count)])
    full = lax.all_gather(mine, "seq", axis=0, tiled=False)
    return full.transpose(1, 0, 2).reshape(value.shape), got[:, width:].astype(extra.dtype)


def summed_to_all(value):
    devices = lax.axis_size("seq")
    chunks = value.astype(jnp.bfloat16).reshape(devices, -1, value.shape[-1])
    got = lax.all_to_all(chunks, "seq", 0, 0, tiled=True)
    total = jnp.sum(got.astype(jnp.float32), axis=0).astype(jnp.bfloat16)
    full = lax.all_gather(total, "seq", axis=0, tiled=True)
    return full.reshape(value.shape).astype(jnp.float32)


def head_blocks(matrix, blocks):
    return matrix.reshape(blocks, BLK, H, HD).transpose(0, 2, 1, 3)


def token_rows(blocked):
    blocks = blocked.shape[0]
    return blocked.transpose(0, 2, 1, 3).reshape(blocks * BLK, H * HD)


def pair_heads(rows, blocks):
    return (
        rows.reshape(blocks, BLK, 2, H, HD).transpose(0, 3, 1, 2, 4).reshape(blocks, H, BLK, 2 * HD)
    )


def slot_plan(block_lists, per_dev, devices, head_ids):
    owners = (block_lists // per_dev).reshape(-1)
    req_codes = (block_lists % per_dev * H + head_ids[None, :, None]).reshape(-1)
    onehot = (owners[:, None] == jnp.arange(devices, dtype=jnp.int32)[None, :]).astype(jnp.int32)
    before = jnp.cumsum(onehot, axis=0) - onehot
    return (owners, jnp.sum(before * onehot, axis=1), req_codes)


def sparse_group(query_g, grad_g, keyvals, allowed, factor):
    key_part = keyvals[..., :HD]
    value_part = keyvals[..., HD:]
    scores = (
        jnp.einsum("ghqd,ghkd->ghqk", query_g, key_part, preferred_element_type=jnp.float32)
        * factor
    )
    mask = allowed[:, :, None, :]
    row_max = jnp.max(jnp.where(mask, scores, -1e30), axis=-1, keepdims=True)
    expo = jnp.where(mask, jnp.exp(scores - row_max), 0.0)
    totals = jnp.sum(expo, axis=-1, keepdims=True)
    result = (
        jnp.einsum(
            "ghqk,ghkd->ghqd",
            expo.astype(jnp.bfloat16),
            value_part,
            preferred_element_type=jnp.float32,
        )
        / totals
    )
    probs = expo / totals
    dprobs = jnp.einsum("ghqd,ghkd->ghqk", grad_g, value_part, preferred_element_type=jnp.float32)
    dotted = jnp.sum(grad_g.astype(jnp.float32) * result, axis=-1, keepdims=True)
    dscore = (probs * (dprobs - dotted)).astype(jnp.bfloat16)
    dquery = factor * jnp.einsum(
        "ghqk,ghkd->ghqd", dscore, key_part, preferred_element_type=jnp.float32
    )
    dkey = factor * jnp.einsum(
        "ghqk,ghqd->ghkd", dscore, query_g, preferred_element_type=jnp.float32
    )
    dvalue = jnp.einsum(
        "ghqk,ghqd->ghkd", probs.astype(jnp.bfloat16), grad_g, preferred_element_type=jnp.float32
    )
    stats = jnp.stack([row_max[..., 0], totals[..., 0], dotted[..., 0]], axis=1)
    return (result, dquery, jnp.concatenate([dkey, dvalue], axis=-1), stats)


def sparse_kernel(q_ref, g_ref, kv_ref, allow_ref, out_ref, dq_ref, win_ref, glob_ref, rand_ref, *, factor):
    nt = (((1,), (1,)), ((), ()))
    for head in range(q_ref.shape[1]):
        query = q_ref[0, head]
        grad = g_ref[0, head]
        keyval = kv_ref[0, head]
        key = keyval[:, :HD]
        value = keyval[:, HD:]
        scores = lax.dot_general(query, key, nt, preferred_element_type=jnp.float32) * factor
        mask = allow_ref[0, head] > 0.5
        row_max = jnp.max(jnp.where(mask, scores, -1e30), axis=-1, keepdims=True)
        expo = jnp.where(mask, jnp.exp(scores - row_max), 0.0)
        totals = jnp.sum(expo, axis=-1, keepdims=True)
        result = (
            jnp.dot(expo.astype(jnp.bfloat16), value, preferred_element_type=jnp.float32)
            / totals
        )
        probs = expo / totals
        dprobs = lax.dot_general(grad, value, nt, preferred_element_type=jnp.float32)
        dotted = jnp.sum(grad.astype(jnp.float32) * result, axis=-1, keepdims=True)
        dscore = probs * (dprobs - dotted)
        dq = factor * jnp.dot(dscore.astype(jnp.bfloat16), key, preferred_element_type=jnp.float32)
        dkey = factor * jnp.dot(
            dscore.astype(jnp.bfloat16).T, query, preferred_element_type=jnp.float32
        )
        dvalue = jnp.dot(probs.astype(jnp.bfloat16).T, grad, preferred_element_type=jnp.float32)
        out_ref[0, head] = result
        dq_ref[0, head] = dq
        kinds = ((win_ref, 0, jnp.float32), (glob_ref, 3, jnp.float32), (rand_ref, 5, jnp.bfloat16))
        for target, first, kind in kinds:
            for slot in range(target.shape[2]):
                rows = slice((first + slot) * BLK, (first + slot + 1) * BLK)
                target[0, head, slot, :, :HD] = dkey[rows].astype(kind)
                target[0, head, slot, :, HD:] = dvalue[rows].astype(kind)


def sparse_call(query_h, grad_h, keyvals, allowed_f, factor, interpret=False, per_step=6):
    blocks, heads, rows, _ = query_h.shape
    keys_n = keyvals.shape[2]
    small = pl.BlockSpec((1, per_step, rows, HD), lambda i, h: (i, h, 0, 0))
    return pl.pallas_call(
        lambda *refs: sparse_kernel(*refs, factor=factor),
        grid=(blocks, heads // per_step),
        in_specs=[
            small,
            small,
            pl.BlockSpec((1, per_step, keys_n, 2 * HD), lambda i, h: (i, h, 0, 0)),
            pl.BlockSpec((1, per_step, 1, keys_n), lambda i, h: (i, h, 0, 0)),
        ],
        out_specs=[
            small,
            small,
            pl.BlockSpec((1, per_step, 3, BLK, 2 * HD), lambda i, h: (i, h, 0, 0, 0)),
            pl.BlockSpec((1, per_step, NG, BLK, 2 * HD), lambda i, h: (i, h, 0, 0, 0)),
            pl.BlockSpec((1, per_step, R, BLK, 2 * HD), lambda i, h: (i, h, 0, 0, 0)),
        ],
        out_shape=[
            jax.ShapeDtypeStruct((blocks, heads, rows, HD), jnp.float32),
            jax.ShapeDtypeStruct((blocks, heads, rows, HD), jnp.float32),
            jax.ShapeDtypeStruct((blocks, heads, 3, BLK, 2 * HD), jnp.float32),
            jax.ShapeDtypeStruct((blocks, heads, NG, BLK, 2 * HD), jnp.float32),
            jax.ShapeDtypeStruct((blocks, heads, R, BLK, 2 * HD), jnp.bfloat16),
        ],
        interpret=interpret,
    )(query_h, grad_h, keyvals, allowed_f)


def per_device(queries, keys, values, out_grad, random_blocks, global_blocks):
    tokens = queries.shape[0]
    width = queries.shape[1]
    per_dev = tokens // BLK
    devices = lax.axis_size("seq")
    me_index = lax.axis_index("seq")
    blocks_all = per_dev * devices
    factor = 1.0 / math.sqrt(HD)
    entry_count = per_dev * H * R
    capacity = (entry_count + devices - 2) // (devices - 1) + 4
    head_ids = jnp.arange(H, dtype=jnp.int32)
    block_ids = me_index * per_dev + jnp.arange(per_dev, dtype=jnp.int32)
    is_global = jnp.any(block_ids[:, None] == global_blocks[None, :], axis=1)
    row_global = jnp.repeat(is_global, BLK)
    masked = jnp.where(row_global[:, None], jnp.zeros_like(out_grad), out_grad)
    kv_rows = jnp.concatenate([keys, values], axis=1)
    edge_rows = jnp.concatenate([kv_rows[:BLK], kv_rows[-BLK:]], axis=0)
    padded = padded_2(edge_rows, (("seq", 0),), BLK)
    left_rows = padded[:BLK]
    right_rows = padded[3 * BLK :]
    extended = jnp.concatenate(
        [
            left_rows[None, :, : 2 * width],
            kv_rows.reshape(per_dev, BLK, 2 * width),
            right_rows[None, :, : 2 * width],
        ],
        axis=0,
    )
    kv_heads = pair_heads(extended, per_dev + 2)
    kv_local = kv_heads[1 : per_dev + 1]
    global_rows = []
    for number in range(NG):
        row_start = global_blocks[number] % per_dev * BLK
        global_rows.append(
            jnp.concatenate(
                [
                    lax.dynamic_slice_in_dim(source, row_start, BLK, 0)
                    for source in (queries, keys, values, out_grad)
                ],
                axis=1,
            )
        )
    stacked_rows = jnp.stack(global_rows)
    owners, slot_ids, req_codes = slot_plan(random_blocks, per_dev, devices, head_ids)
    slot_key = owners * capacity + slot_ids
    slot_hit = jnp.arange(devices * capacity, dtype=jnp.int32)[:, None] == slot_key[None, :]
    outgoing = jnp.where(
        jnp.any(slot_hit, axis=1), jnp.sum(jnp.where(slot_hit, req_codes[None, :], 0), axis=1), -1
    ).reshape(devices, capacity)
    grows, wanted = from_owners(stacked_rows, global_blocks // per_dev, outgoing)
    sending = kv_local.reshape(per_dev * H, BLK, 2 * HD)[jnp.maximum(wanted, 0)]
    g_query = grows[:, :, :width].reshape(NG, BLK, H, HD)
    g_grad = grows[:, :, 3 * width :].reshape(NG, BLK, H, HD)
    g_kv = pair_heads(grows[:, :, width : 3 * width], NG)
    fetched = lax.all_to_all(sending, "seq", split_axis=0, concat_axis=0, tiled=True)
    rand_kv = fetched[owners, slot_ids].reshape(per_dev, H, R, BLK, 2 * HD)
    shifts = jnp.arange(-1, 2, dtype=jnp.int32)
    window_ids = (block_ids[:, None] + shifts[None, :]) % blocks_all
    other_ids = jnp.concatenate(
        [jnp.broadcast_to(window_ids[:, None, :], (per_dev, H, 3)), random_blocks], axis=2
    )
    global_kept = jnp.all(global_blocks[None, None, :, None] != other_ids[:, :, None, :], axis=3)
    allowed = jnp.concatenate(
        [jnp.ones((per_dev, H, 3), jnp.bool_), global_kept, jnp.ones((per_dev, H, R), jnp.bool_)],
        axis=2,
    )
    allowed = jnp.repeat(allowed, BLK, axis=2)
    query_heads = head_blocks(queries, per_dev)
    grad_heads = head_blocks(masked, per_dev)
    group = QGROUP
    groups = per_dev // group
    glob_slots = jnp.broadcast_to(g_kv.transpose(1, 0, 2, 3)[None], (group, H, NG, BLK, 2 * HD))

    def run_group(number):
        win_slots = jnp.stack(
            [kv_heads[0:group], kv_heads[1 : group + 1], kv_heads[2 : group + 2]], axis=2
        )
        keyvals = jnp.concatenate([win_slots, glob_slots, rand_kv], axis=2).reshape(
            group, H, SLOTS * BLK, 2 * HD
        )
        result, dquery, win_terms, glob_terms, random_out = sparse_call(
            query_heads, grad_heads, keyvals, allowed.astype(jnp.float32)[:, :, None, :], factor
        )
        spacing = ((0, 0), (0, 0), (0, 0), (0, 0))
        window_sum = (
            jnp.pad(win_terms[:, :, 0], ((0, 2),) + spacing[1:])
            + jnp.pad(win_terms[:, :, 1], ((1, 1),) + spacing[1:])
            + jnp.pad(win_terms[:, :, 2], ((2, 0),) + spacing[1:])
        )
        global_sum = jnp.sum(glob_terms, axis=0)
        return (result, dquery, window_sum, global_sum, random_out)

    if groups == 1:
        mapped = tuple(part[None] for part in run_group(0))
    else:
        mapped = lax.map(run_group, jnp.arange(groups, dtype=jnp.int32))
    result = mapped[0].reshape(per_dev, H, BLK, HD)
    dquery = mapped[1].reshape(per_dev, H, BLK, HD)
    place = (
        jnp.arange(groups, dtype=jnp.int32)[:, None] * group
        + jnp.arange(group + 2, dtype=jnp.int32)[None, :]
    ).reshape(-1)
    if groups == 1:
        padded_grads = mapped[2].reshape(per_dev + 2, H, BLK, 2 * HD)
    else:
        padded_grads = (
            jnp.zeros((per_dev + 2, H, BLK, 2 * HD), jnp.float32)
            .at[place]
            .add(mapped[2].reshape(-1, H, BLK, 2 * HD))
        )
    global_part = jnp.sum(mapped[3], axis=0).transpose(1, 0, 2, 3)
    random_out = mapped[4].reshape(-1, BLK, 2 * HD)
    own_grads = padded_grads[1 : per_dev + 1]
    edge_pair = jnp.stack([padded_grads[0], padded_grads[per_dev + 1]])
    near_grads = padded_2(edge_pair.astype(jnp.bfloat16), (("seq", 0),), 1).astype(edge_pair.dtype)
    own_grads = own_grads.at[0].add(near_grads[0]).at[per_dev - 1].add(near_grads[3])
    back_buffer = jnp.einsum(
        "se,ef->sf",
        slot_hit.astype(jnp.bfloat16),
        random_out.reshape(-1, BLK * 2 * HD),
        preferred_element_type=jnp.bfloat16,
    ).reshape(devices, capacity, BLK, 2 * HD)
    returned = lax.all_to_all(back_buffer, "seq", split_axis=0, concat_axis=0, tiled=True)
    code_hit = (
        wanted.reshape(-1)[:, None] == jnp.arange(per_dev * H, dtype=jnp.int32)[None, :]
    ).astype(jnp.bfloat16)
    table_grads = jnp.einsum(
        "sc,sf->cf",
        code_hit,
        returned.reshape(-1, BLK * 2 * HD),
        preferred_element_type=jnp.float32,
    ).reshape(per_dev * H, BLK, 2 * HD)
    own_grads = own_grads + table_grads.reshape(per_dev, H, BLK, 2 * HD)
    key_tok = keys.reshape(tokens, H, HD)
    value_tok = values.reshape(tokens, H, HD)
    scores = (
        jnp.einsum("gqhd,khd->ghqk", g_query, key_tok, preferred_element_type=jnp.float32) * factor
    )
    local_max = jnp.max(scores, axis=-1)
    local_expo = jnp.exp(scores - local_max[..., None])
    part_acc = jnp.einsum(
        "ghqk,khd->ghqd",
        local_expo.astype(jnp.bfloat16),
        value_tok,
        preferred_element_type=jnp.float32,
    )
    row_shape = local_max.shape
    packed = jnp.concatenate(
        [local_max[..., None], jnp.sum(local_expo, axis=-1)[..., None], part_acc], axis=-1
    ).reshape(devices, -1, HD + 2)
    got = lax.all_to_all(packed, "seq", 0, 0, tiled=True)
    top = jnp.max(got[..., 0], axis=0)
    scale = jnp.exp(got[..., 0] - top[None])
    tot = jnp.sum(scale * got[..., 1], axis=0)
    acc = jnp.sum(scale[..., None] * got[..., 2:], axis=0) / tot[:, None]
    merged = lax.all_gather(
        jnp.concatenate([top[:, None], tot[:, None], acc], axis=-1), "seq", axis=0, tiled=True
    )
    row_top = merged[:, 0].reshape(row_shape)
    row_tot = merged[:, 1].reshape(row_shape)
    global_out = merged[:, 2:].reshape(row_shape + (HD,))
    probs = jnp.exp(scores - row_top[..., None]) / row_tot[..., None]
    dprobs = jnp.einsum("gqhd,khd->ghqk", g_grad, value_tok, preferred_element_type=jnp.float32)
    dotted = jnp.sum(g_grad.transpose(0, 2, 1, 3).astype(jnp.float32) * global_out, axis=-1)
    dscore = (probs * (dprobs - dotted[..., None])).astype(jnp.bfloat16)
    g_dquery = factor * jnp.einsum(
        "ghqk,khd->ghqd", dscore, key_tok, preferred_element_type=jnp.float32
    )
    tok_dkey = factor * jnp.einsum(
        "ghqk,gqhd->khd", dscore, g_query, preferred_element_type=jnp.float32
    )
    tok_dvalue = jnp.einsum(
        "ghqk,gqhd->khd", probs.astype(jnp.bfloat16), g_grad, preferred_element_type=jnp.float32
    )
    both_sum = summed_to_all(jnp.concatenate([g_dquery, global_part], axis=-1))
    dquery_sum = both_sum[..., :HD]
    global_sum = both_sum[..., HD:]
    for number in range(NG):
        owned = global_blocks[number] // per_dev == me_index
        local_block = global_blocks[number] % per_dev
        result = result.at[local_block].set(
            jnp.where(owned, global_out[number], result[local_block])
        )
        dquery = dquery.at[local_block].add(jnp.where(owned, dquery_sum[number], 0.0))
        own_grads = own_grads.at[local_block].add(jnp.where(owned, global_sum[number], 0.0))
    attended = token_rows(result).astype(jnp.bfloat16)
    query_grad = token_rows(dquery).astype(jnp.bfloat16)
    key_grad = (token_rows(own_grads[..., :HD]) + tok_dkey.reshape(tokens, width)).astype(
        jnp.bfloat16
    )
    value_grad = (token_rows(own_grads[..., HD:]) + tok_dvalue.reshape(tokens, width)).astype(
        jnp.bfloat16
    )
    return (attended, query_grad, key_grad, value_grad)


def solution(mesh):
    return jax.shard_map(
        per_device,
        mesh=mesh,
        in_specs=(
            P(("grp", "seq"), None),
            P(("grp", "seq"), None),
            P(("grp", "seq"), None),
            P(("grp", "seq"), None),
            P(("grp", "seq"), None, None),
            P("grp"),
        ),
        out_specs=(
            P(("grp", "seq"), None),
            P(("grp", "seq"), None),
            P(("grp", "seq"), None),
            P(("grp", "seq"), None),
        ),
        check_vma=False,
    )
```

```python
import math

import jax
import jax.numpy as jnp
from jax import lax
from jax.experimental import pallas as pl
from jax.sharding import PartitionSpec as P

H = 12
HD = 64
BLK = 64
R = 3
NG = 2
QGROUP = 8
SLOTS = 8


def padded_2(block, sides, width):
    for axis, dim in sides:
        count = lax.axis_size(axis)
        forward = [(i, i + 1) for i in range(count - 1)]
        forward.append((count - 1, 0))
        backward = [(target, source) for source, target in forward]
        low = lax.ppermute(
            lax.slice_in_dim(block, block.shape[dim] - width, None, axis=dim), axis, forward
        )
        high = lax.ppermute(lax.slice_in_dim(block, 0, width, axis=dim), axis, backward)
        block = jnp.concatenate([low, block, high], axis=dim)
    return block


def from_owners(value, owners, extra):
    devices = lax.axis_size("seq")
    count, rows_all, width = value.shape
    per = rows_all // devices
    chunks = value.reshape(count, devices, per, width).transpose(1, 0, 2, 3)
    chunks = chunks.reshape(devices, count * per, width)
    side = jnp.pad(extra.astype(value.dtype), ((0, 0), (0, width - extra.shape[1])))
    got = lax.all_to_all(
        jnp.concatenate([chunks, side[:, None, :]], axis=1), "seq", 0, 0, tiled=True
    )
    rows = got[:, : count * per].reshape(devices, count, per, width)
    mine = jnp.stack([rows[owners[i], i] for i in range(count)])
    full = lax.all_gather(mine, "seq", axis=0, tiled=False)
    wanted = got[:, count * per, : extra.shape[1]].astype(extra.dtype)
    return full.transpose(1, 0, 2, 3).reshape(value.shape), wanted


def summed_to_all(value):
    devices = lax.axis_size("seq")
    chunks = value.astype(jnp.bfloat16).reshape(devices, -1, value.shape[-1])
    got = lax.all_to_all(chunks, "seq", 0, 0, tiled=True)
    total = jnp.sum(got.astype(jnp.float32), axis=0).astype(jnp.bfloat16)
    full = lax.all_gather(total, "seq", axis=0, tiled=True)
    return full.reshape(value.shape).astype(jnp.float32)


def head_blocks(matrix, blocks):
    return matrix.reshape(blocks, BLK, H, HD).transpose(0, 2, 1, 3)


def token_rows(blocked):
    blocks = blocked.shape[0]
    return blocked.transpose(0, 2, 1, 3).reshape(blocks * BLK, H * HD)


def pair_heads(rows, blocks):
    return (
        rows.reshape(blocks, BLK, 2, H, HD).transpose(0, 3, 1, 2, 4).reshape(blocks, H, BLK, 2 * HD)
    )


def slot_plan(block_lists, per_dev, devices, head_ids):
    owners = (block_lists // per_dev).reshape(-1)
    req_codes = (block_lists % per_dev * H + head_ids[None, :, None]).reshape(-1)
    onehot = (owners[:, None] == jnp.arange(devices, dtype=jnp.int32)[None, :]).astype(jnp.int32)
    before = jnp.cumsum(onehot, axis=0) - onehot
    return (owners, jnp.sum(before * onehot, axis=1), req_codes)


def sparse_group(query_g, grad_g, keyvals, allowed, factor):
    key_part = keyvals[..., :HD]
    value_part = keyvals[..., HD:]
    scores = (
        jnp.einsum("ghqd,ghkd->ghqk", query_g, key_part, preferred_element_type=jnp.float32)
        * factor
    )
    mask = allowed[:, :, None, :]
    row_max = jnp.max(jnp.where(mask, scores, -1e30), axis=-1, keepdims=True)
    expo = jnp.where(mask, jnp.exp(scores - row_max), 0.0)
    totals = jnp.sum(expo, axis=-1, keepdims=True)
    result = (
        jnp.einsum(
            "ghqk,ghkd->ghqd",
            expo.astype(jnp.bfloat16),
            value_part,
            preferred_element_type=jnp.float32,
        )
        / totals
    )
    probs = expo / totals
    dprobs = jnp.einsum("ghqd,ghkd->ghqk", grad_g, value_part, preferred_element_type=jnp.float32)
    dotted = jnp.sum(grad_g.astype(jnp.float32) * result, axis=-1, keepdims=True)
    dscore = (probs * (dprobs - dotted)).astype(jnp.bfloat16)
    dquery = factor * jnp.einsum(
        "ghqk,ghkd->ghqd", dscore, key_part, preferred_element_type=jnp.float32
    )
    dkey = factor * jnp.einsum(
        "ghqk,ghqd->ghkd", dscore, query_g, preferred_element_type=jnp.float32
    )
    dvalue = jnp.einsum(
        "ghqk,ghqd->ghkd", probs.astype(jnp.bfloat16), grad_g, preferred_element_type=jnp.float32
    )
    stats = jnp.stack([row_max[..., 0], totals[..., 0], dotted[..., 0]], axis=1)
    return (result, dquery, jnp.concatenate([dkey, dvalue], axis=-1), stats)


def sparse_kernel(q_ref, g_ref, kv_ref, allow_ref, out_ref, dq_ref, win_ref, glob_ref, rand_ref, *, factor):
    nt = (((1,), (1,)), ((), ()))
    for head in range(q_ref.shape[1]):
        query = q_ref[0, head]
        grad = g_ref[0, head]
        keyval = kv_ref[0, head]
        key = keyval[:, :HD]
        value = keyval[:, HD:]
        scores = lax.dot_general(query, key, nt, preferred_element_type=jnp.float32) * factor
        mask = allow_ref[0, head] > 0.5
        row_max = jnp.max(jnp.where(mask, scores, -1e30), axis=-1, keepdims=True)
        expo = jnp.where(mask, jnp.exp(scores - row_max), 0.0)
        totals = jnp.sum(expo, axis=-1, keepdims=True)
        result = (
            jnp.dot(expo.astype(jnp.bfloat16), value, preferred_element_type=jnp.float32)
            / totals
        )
        probs = expo / totals
        dprobs = lax.dot_general(grad, value, nt, preferred_element_type=jnp.float32)
        dotted = jnp.sum(grad.astype(jnp.float32) * result, axis=-1, keepdims=True)
        dscore = probs * (dprobs - dotted)
        dq = factor * jnp.dot(dscore.astype(jnp.bfloat16), key, preferred_element_type=jnp.float32)
        dkey = factor * jnp.dot(
            dscore.astype(jnp.bfloat16).T, query, preferred_element_type=jnp.float32
        )
        dvalue = jnp.dot(probs.astype(jnp.bfloat16).T, grad, preferred_element_type=jnp.float32)
        out_ref[0, head] = result
        dq_ref[0, head] = dq
        kinds = ((win_ref, 0, jnp.float32), (glob_ref, 3, jnp.float32), (rand_ref, 5, jnp.bfloat16))
        for target, first, kind in kinds:
            for slot in range(target.shape[2]):
                rows = slice((first + slot) * BLK, (first + slot + 1) * BLK)
                target[0, head, slot, :, :HD] = dkey[rows].astype(kind)
                target[0, head, slot, :, HD:] = dvalue[rows].astype(kind)


def sparse_call(query_h, grad_h, keyvals, allowed_f, factor, interpret=False, per_step=6):
    blocks, heads, rows, _ = query_h.shape
    keys_n = keyvals.shape[2]
    small = pl.BlockSpec((1, per_step, rows, HD), lambda i, h: (i, h, 0, 0))
    return pl.pallas_call(
        lambda *refs: sparse_kernel(*refs, factor=factor),
        grid=(blocks, heads // per_step),
        in_specs=[
            small,
            small,
            pl.BlockSpec((1, per_step, keys_n, 2 * HD), lambda i, h: (i, h, 0, 0)),
            pl.BlockSpec((1, per_step, 1, keys_n), lambda i, h: (i, h, 0, 0)),
        ],
        out_specs=[
            small,
            small,
            pl.BlockSpec((1, per_step, 3, BLK, 2 * HD), lambda i, h: (i, h, 0, 0, 0)),
            pl.BlockSpec((1, per_step, NG, BLK, 2 * HD), lambda i, h: (i, h, 0, 0, 0)),
            pl.BlockSpec((1, per_step, R, BLK, 2 * HD), lambda i, h: (i, h, 0, 0, 0)),
        ],
        out_shape=[
            jax.ShapeDtypeStruct((blocks, heads, rows, HD), jnp.float32),
            jax.ShapeDtypeStruct((blocks, heads, rows, HD), jnp.float32),
            jax.ShapeDtypeStruct((blocks, heads, 3, BLK, 2 * HD), jnp.float32),
            jax.ShapeDtypeStruct((blocks, heads, NG, BLK, 2 * HD), jnp.float32),
            jax.ShapeDtypeStruct((blocks, heads, R, BLK, 2 * HD), jnp.bfloat16),
        ],
        interpret=interpret,
    )(query_h, grad_h, keyvals, allowed_f)


def per_device(queries, keys, values, out_grad, random_blocks, global_blocks):
    tokens = queries.shape[0]
    width = queries.shape[1]
    per_dev = tokens // BLK
    devices = lax.axis_size("seq")
    me_index = lax.axis_index("seq")
    blocks_all = per_dev * devices
    factor = 1.0 / math.sqrt(HD)
    entry_count = per_dev * H * R
    capacity = (entry_count + devices - 2) // (devices - 1) + 4
    head_ids = jnp.arange(H, dtype=jnp.int32)
    block_ids = me_index * per_dev + jnp.arange(per_dev, dtype=jnp.int32)
    is_global = jnp.any(block_ids[:, None] == global_blocks[None, :], axis=1)
    row_global = jnp.repeat(is_global, BLK)
    masked = jnp.where(row_global[:, None], jnp.zeros_like(out_grad), out_grad)
    kv_rows = jnp.concatenate([keys, values], axis=1)
    edge_rows = jnp.concatenate([kv_rows[:BLK], kv_rows[-BLK:]], axis=0)
    padded = padded_2(edge_rows, (("seq", 0),), BLK)
    left_rows = padded[:BLK]
    right_rows = padded[3 * BLK :]
    extended = jnp.concatenate(
        [
            left_rows[None, :, : 2 * width],
            kv_rows.reshape(per_dev, BLK, 2 * width),
            right_rows[None, :, : 2 * width],
        ],
        axis=0,
    )
    kv_heads = pair_heads(extended, per_dev + 2)
    kv_local = kv_heads[1 : per_dev + 1]
    global_rows = []
    for number in range(NG):
        row_start = global_blocks[number] % per_dev * BLK
        global_rows.append(
            jnp.concatenate(
                [
                    lax.dynamic_slice_in_dim(source, row_start, BLK, 0)
                    for source in (queries, keys, values, out_grad)
                ],
                axis=1,
            )
        )
    stacked_rows = jnp.stack(global_rows)
    owners, slot_ids, req_codes = slot_plan(random_blocks, per_dev, devices, head_ids)
    slot_key = owners * capacity + slot_ids
    slot_hit = jnp.arange(devices * capacity, dtype=jnp.int32)[:, None] == slot_key[None, :]
    outgoing = jnp.where(
        jnp.any(slot_hit, axis=1), jnp.sum(jnp.where(slot_hit, req_codes[None, :], 0), axis=1), -1
    ).reshape(devices, capacity)
    grows, wanted = from_owners(stacked_rows, global_blocks // per_dev, outgoing)
    sending = kv_local.reshape(per_dev * H, BLK, 2 * HD)[jnp.maximum(wanted, 0)]
    g_query = grows[:, :, :width].reshape(NG, BLK, H, HD)
    g_grad = grows[:, :, 3 * width :].reshape(NG, BLK, H, HD)
    g_kv = pair_heads(grows[:, :, width : 3 * width], NG)
    fetched = lax.all_to_all(sending, "seq", split_axis=0, concat_axis=0, tiled=True)
    rand_kv = fetched[owners, slot_ids].reshape(per_dev, H, R, BLK, 2 * HD)
    shifts = jnp.arange(-1, 2, dtype=jnp.int32)
    window_ids = (block_ids[:, None] + shifts[None, :]) % blocks_all
    other_ids = jnp.concatenate(
        [jnp.broadcast_to(window_ids[:, None, :], (per_dev, H, 3)), random_blocks], axis=2
    )
    global_kept = jnp.all(global_blocks[None, None, :, None] != other_ids[:, :, None, :], axis=3)
    allowed = jnp.concatenate(
        [jnp.ones((per_dev, H, 3), jnp.bool_), global_kept, jnp.ones((per_dev, H, R), jnp.bool_)],
        axis=2,
    )
    allowed = jnp.repeat(allowed, BLK, axis=2)
    query_heads = head_blocks(queries, per_dev)
    grad_heads = head_blocks(masked, per_dev)
    group = QGROUP
    groups = per_dev // group
    glob_slots = jnp.broadcast_to(g_kv.transpose(1, 0, 2, 3)[None], (group, H, NG, BLK, 2 * HD))

    def run_group(number):
        win_slots = jnp.stack(
            [kv_heads[0:group], kv_heads[1 : group + 1], kv_heads[2 : group + 2]], axis=2
        )
        keyvals = jnp.concatenate([win_slots, glob_slots, rand_kv], axis=2).reshape(
            group, H, SLOTS * BLK, 2 * HD
        )
        result, dquery, win_terms, glob_terms, random_out = sparse_call(
            query_heads, grad_heads, keyvals, allowed.astype(jnp.float32)[:, :, None, :], factor
        )
        spacing = ((0, 0), (0, 0), (0, 0), (0, 0))
        window_sum = (
            jnp.pad(win_terms[:, :, 0], ((0, 2),) + spacing[1:])
            + jnp.pad(win_terms[:, :, 1], ((1, 1),) + spacing[1:])
            + jnp.pad(win_terms[:, :, 2], ((2, 0),) + spacing[1:])
        )
        global_sum = jnp.sum(glob_terms, axis=0)
        return (result, dquery, window_sum, global_sum, random_out)

    if groups == 1:
        mapped = tuple(part[None] for part in run_group(0))
    else:
        mapped = lax.map(run_group, jnp.arange(groups, dtype=jnp.int32))
    result = mapped[0].reshape(per_dev, H, BLK, HD)
    dquery = mapped[1].reshape(per_dev, H, BLK, HD)
    place = (
        jnp.arange(groups, dtype=jnp.int32)[:, None] * group
        + jnp.arange(group + 2, dtype=jnp.int32)[None, :]
    ).reshape(-1)
    if groups == 1:
        padded_grads = mapped[2].reshape(per_dev + 2, H, BLK, 2 * HD)
    else:
        padded_grads = (
            jnp.zeros((per_dev + 2, H, BLK, 2 * HD), jnp.float32)
            .at[place]
            .add(mapped[2].reshape(-1, H, BLK, 2 * HD))
        )
    global_part = jnp.sum(mapped[3], axis=0).transpose(1, 0, 2, 3)
    random_out = mapped[4].reshape(-1, BLK, 2 * HD)
    own_grads = padded_grads[1 : per_dev + 1]
    edge_pair = jnp.stack([padded_grads[0], padded_grads[per_dev + 1]])
    near_grads = padded_2(edge_pair.astype(jnp.bfloat16), (("seq", 0),), 1).astype(edge_pair.dtype)
    own_grads = own_grads.at[0].add(near_grads[0]).at[per_dev - 1].add(near_grads[3])
    back_buffer = jnp.einsum(
        "se,ef->sf",
        slot_hit.astype(jnp.bfloat16),
        random_out.reshape(-1, BLK * 2 * HD),
        preferred_element_type=jnp.bfloat16,
    ).reshape(devices, capacity, BLK, 2 * HD)
    returned = lax.all_to_all(back_buffer, "seq", split_axis=0, concat_axis=0, tiled=True)
    code_hit = (
        wanted.reshape(-1)[:, None] == jnp.arange(per_dev * H, dtype=jnp.int32)[None, :]
    ).astype(jnp.bfloat16)
    table_grads = jnp.einsum(
        "sc,sf->cf",
        code_hit,
        returned.reshape(-1, BLK * 2 * HD),
        preferred_element_type=jnp.float32,
    ).reshape(per_dev * H, BLK, 2 * HD)
    own_grads = own_grads + table_grads.reshape(per_dev, H, BLK, 2 * HD)
    key_tok = keys.reshape(tokens, H, HD)
    value_tok = values.reshape(tokens, H, HD)
    scores = (
        jnp.einsum("gqhd,khd->ghqk", g_query, key_tok, preferred_element_type=jnp.float32) * factor
    )
    local_max = jnp.max(scores, axis=-1)
    local_expo = jnp.exp(scores - local_max[..., None])
    part_acc = jnp.einsum(
        "ghqk,khd->ghqd",
        local_expo.astype(jnp.bfloat16),
        value_tok,
        preferred_element_type=jnp.float32,
    )
    row_shape = local_max.shape
    packed = jnp.concatenate(
        [local_max[..., None], jnp.sum(local_expo, axis=-1)[..., None], part_acc], axis=-1
    ).reshape(devices, -1, HD + 2)
    got = lax.all_to_all(packed, "seq", 0, 0, tiled=True)
    top = jnp.max(got[..., 0], axis=0)
    scale = jnp.exp(got[..., 0] - top[None])
    tot = jnp.sum(scale * got[..., 1], axis=0)
    acc = jnp.sum(scale[..., None] * got[..., 2:], axis=0) / tot[:, None]
    merged = lax.all_gather(
        jnp.concatenate([top[:, None], tot[:, None], acc], axis=-1), "seq", axis=0, tiled=True
    )
    row_top = merged[:, 0].reshape(row_shape)
    row_tot = merged[:, 1].reshape(row_shape)
    global_out = merged[:, 2:].reshape(row_shape + (HD,))
    probs = jnp.exp(scores - row_top[..., None]) / row_tot[..., None]
    dprobs = jnp.einsum("gqhd,khd->ghqk", g_grad, value_tok, preferred_element_type=jnp.float32)
    dotted = jnp.sum(g_grad.transpose(0, 2, 1, 3).astype(jnp.float32) * global_out, axis=-1)
    dscore = (probs * (dprobs - dotted[..., None])).astype(jnp.bfloat16)
    g_dquery = factor * jnp.einsum(
        "ghqk,khd->ghqd", dscore, key_tok, preferred_element_type=jnp.float32
    )
    tok_dkey = factor * jnp.einsum(
        "ghqk,gqhd->khd", dscore, g_query, preferred_element_type=jnp.float32
    )
    tok_dvalue = jnp.einsum(
        "ghqk,gqhd->khd", probs.astype(jnp.bfloat16), g_grad, preferred_element_type=jnp.float32
    )
    both_sum = summed_to_all(jnp.concatenate([g_dquery, global_part], axis=-1))
    dquery_sum = both_sum[..., :HD]
    global_sum = both_sum[..., HD:]
    for number in range(NG):
        owned = global_blocks[number] // per_dev == me_index
        local_block = global_blocks[number] % per_dev
        result = result.at[local_block].set(
            jnp.where(owned, global_out[number], result[local_block])
        )
        dquery = dquery.at[local_block].add(jnp.where(owned, dquery_sum[number], 0.0))
        own_grads = own_grads.at[local_block].add(jnp.where(owned, global_sum[number], 0.0))
    attended = token_rows(result).astype(jnp.bfloat16)
    query_grad = token_rows(dquery).astype(jnp.bfloat16)
    key_grad = (token_rows(own_grads[..., :HD]) + tok_dkey.reshape(tokens, width)).astype(
        jnp.bfloat16
    )
    value_grad = (token_rows(own_grads[..., HD:]) + tok_dvalue.reshape(tokens, width)).astype(
        jnp.bfloat16
    )
    return (attended, query_grad, key_grad, value_grad)


def solution(mesh):
    return jax.shard_map(
        per_device,
        mesh=mesh,
        in_specs=(
            P(("grp", "seq"), None),
            P(("grp", "seq"), None),
            P(("grp", "seq"), None),
            P(("grp", "seq"), None),
            P(("grp", "seq"), None, None),
            P("grp"),
        ),
        out_specs=(
            P(("grp", "seq"), None),
            P(("grp", "seq"), None),
            P(("grp", "seq"), None),
            P(("grp", "seq"), None),
        ),
        check_vma=False,
    )
```
